32 devices in a mesh: lon: 8 (over y, x, core), lat: 4 (over z).
Axes of the slice: x: 2, y: 2, z: 4, core: 2. Of those that a mesh axis runs over, the one named last changes fastest.
Arguments:
- background: bfloat16 [128, 512, 256], P('lat', 'lon'), may hold values from -6 to 6
- observations: bfloat16 [32768, 128], P(('lon', 'lat')), may hold values from -6 to 6
- w_station: bfloat16 [128, 256], replicated, may hold values from -0.5 to 0.5
- w_first: bfloat16 [3, 3, 256, 256], replicated, may hold values from -0.125 to 0.125
- w_second: bfloat16 [4, 4, 256, 256], replicated, may hold values from -0.09375 to 0.09375
- cotangent: bfloat16 [64, 256, 256], P('lat', 'lon'), may hold values from -6 to 6
- station_tile: int32 [32768, 1], P(('lon', 'lat')), may hold values from 0 to 31; in each aligned block of 1024 rows (0 to 1023, 1024 to 2047, ...) at most 64 rows name the same one
- station_cell: int32 [32768], P(('lon', 'lat')), may hold values from 0 to 2047
Outputs:
- encoded: bfloat16 [64, 256, 256], P('lat', 'lon')
- station_grad: bfloat16 [32768, 128], P(('lon', 'lat'))
- weight_grad: float32 [128, 256], replicated
The draws below stay inside these ranges and needn't reach their ends.
Inputs may be any that keep to these rules, and one draw needn't show every extreme that they name: `station_tile`: tiles are numbered in the mesh's device order, longitude index times 4 plus latitude index. Among the 1024 observations that one device holds (aligned blocks), at most 64 name the same tile, and in every draw some device's observations name one tile exactly 64 times. `station_cell`: cell within the observation's tile, row-major over 32 x 64 cells.
All inputs are finite; a program needn't handle non-finite values.
Results may differ from the reference program's by a relative error of at most 0.0061.
Values may be sent and summed in bfloat16 or wider, within the bound.
No kernel may reach another device: no remote copies, remote signals or barrier semaphores. Data moves between devices by JAX's collectives and lax.ppermute only.
A program may use at most 64 MiB of HBM per device.

```python
import math
import jax
import jax.numpy as jnp
import numpy as np
from jax import lax

C = 256
F = 128
LAT_DEV = 32
LON_DEV = 64
S_DEV = 1024
NLAT = 128
NLON = 512
STATIONS = 32768
CAP = 64
TILE_CELLS = 2048
N_LAT = 4
DEVICES = 32


def place_ends(drawn, key, smallest, largest):
    place = [jax.random.randint(jax.random.fold_in(key, axis), (), 0, length) for axis, length in enumerate(drawn.shape)]
    main_axis = drawn.shape.index(max(drawn.shape))
    beside = place[:main_axis] + [(place[main_axis] + 1) % drawn.shape[main_axis]] + place[main_axis + 1:]
    return drawn.at[tuple(place)].set(smallest).at[tuple(beside)].set(largest)


def levels(own_key, shape, split, low, high):
    factor_of, own = 1.0, jax.random.fold_in(own_key, 6)
    for dim, parts in split:
        heights = jnp.exp(jax.random.uniform(jax.random.fold_in(own, dim), (parts,), jnp.float32, low / len(split), high / len(split)))
        factor_of = factor_of * jnp.repeat(heights, shape[dim] // parts).reshape([-1 if axis == dim else 1 for axis in range(len(shape))])
    return factor_of


def deal_out(own_key, own, number, rows, number_of, top, bound, slope):
    ranking = jax.random.permutation(own_key, number_of)
    crowded, usual = load_shares(number_of, rows * top, bound, slope, True), load_shares(number_of, rows * top, bound, slope, False)
    places = jnp.arange(number_of)

    def named(tallies, offset_by):
        used = int((tallies > 0).sum())
        fixed = max(1, used // 4)
        passed = fixed + (places - fixed + offset_by * (used - fixed)) % max(1, number_of - fixed)
        return jnp.zeros((number_of,), jnp.int32).at[ranking[jnp.where(places < fixed, places, passed)]].set(jnp.asarray(tallies, jnp.int32))

    tallies = jnp.where(number % 4 == 0, named(crowded, number // 4), named(usual, number - number // 4 - 1))
    mixed = jax.random.permutation(jax.random.fold_in(own, 3), number_of)
    giver, taker = mixed[0:number_of // 2 * 2:2], mixed[1:number_of // 2 * 2:2]
    room = jnp.minimum(tallies[giver] - 1, bound - tallies[taker]) // 2
    room = jnp.where((giver == ranking[0]) | (taker == ranking[0]) | (tallies[taker] == 0), 0, jnp.maximum(room, 0))
    passed = jax.random.randint(jax.random.fold_in(own, 4), (number_of // 2,), 0, 1 << 20) % (room + 1)
    tallies = tallies.at[giver].add(-passed).at[taker].add(passed)
    items = jnp.searchsorted(jnp.cumsum(tallies), jnp.arange(rows * top), side="right").astype(jnp.int32)
    grid = items.reshape(top, rows).T
    grid = grid[jax.random.permutation(jax.random.fold_in(own, 1), rows)]
    offset_by = jax.random.randint(jax.random.fold_in(own, 2), (rows, 1), 0, top)
    return jnp.take_along_axis(grid, (jnp.arange(top)[None, :] + offset_by) % top, axis=1)


def load_shares(number_of, total, limit, lean, full):
    loads = [(1 << 20) // math.isqrt(grade ** lean) + 1 for grade in range(1, number_of + 1)]
    largest = limit if full else min(limit, max(-(-total // number_of), total * loads[0] // sum(loads)))
    least = 1 if total - largest >= number_of - 1 else 0
    given, spare = [largest] + [least] * (number_of - 1), total - largest - least * (number_of - 1)
    while spare > 0:
        candidates = [i for i in range(1, number_of) if given[i] < largest] or [i for i in range(1, number_of) if given[i] < limit]
        whole, left = sum([loads[i] for i in candidates]), spare
        for i in candidates:
            more = min(limit - given[i], max(1, left * loads[i] // whole), spare)
            given[i] = given[i] + more
            spare = spare - more
    return np.array(given)


def bell_draw(stream_key, shape, spread, bound, split=(), kind=jnp.bfloat16):
    values = jax.random.normal(stream_key, shape, jnp.float32) * spread
    if len(split) > 0:
        values = levels(stream_key, shape, split, -0.22, 0.18) * values
    return jnp.clip(values, min=-bound, max=bound).astype(kind)


def setup_inputs(seed: int = 0) -> dict:
    key_list = jax.random.split(jax.random.key(seed), 9)
    background = bell_draw(key_list[0], (NLAT, NLON, C), 1.0, 6.0, ((0, 4), (1, 8)))
    observations = bell_draw(key_list[1], (STATIONS, F), 1.0, 6.0, ((0, 32),))
    w_station = bell_draw(key_list[2], (F, C), F ** -0.5, 0.5)
    w_first = bell_draw(key_list[3], (3, 3, C, C), (9 * C) ** -0.5, 0.125)
    w_second = bell_draw(key_list[4], (4, 4, C, C), (16 * C) ** -0.5, 0.09375)
    cotangent = bell_draw(key_list[5], (NLAT // 2, NLON // 2, C), 1.0, 6.0, ((0, 4), (1, 8)))
    station_tile_keys = jax.random.split(jax.random.fold_in(key_list[6], 1), STATIONS // S_DEV)
    station_tile_turns = jax.random.permutation(jax.random.fold_in(key_list[6], 3), STATIONS // S_DEV)
    station_tile = jax.vmap(lambda own, number: deal_out(jax.random.fold_in(key_list[6], 2), own, number, S_DEV, DEVICES, 1, CAP, 2))(station_tile_keys, station_tile_turns).reshape((STATIONS, 1))
    station_cell = place_ends(jax.random.randint(key_list[7], (STATIONS,), 0, TILE_CELLS), jax.random.fold_in(key_list[7], 1), 0, TILE_CELLS - 1).astype(jnp.int32)
    return dict(background=background, observations=observations, w_station=w_station, w_first=w_first, w_second=w_second, cotangent=cotangent, station_tile=station_tile, station_cell=station_cell)


def activate(values):
    return jax.nn.gelu(values, approximate=True)

def activate_back(values, upstream):
    return jax.vjp(activate, values)[1](upstream)[0]

def wrap_pad(grid_field):
    lon_sides = jnp.concatenate([grid_field[:, -1:], grid_field, grid_field[:, :1]], axis=1)
    return jnp.pad(lon_sides, ((1, 1), (0, 0), (0, 0)))

def convolve(grid_field, kernel, stride):
    padded = wrap_pad(grid_field)[None]
    result = lax.conv_general_dilated(padded, kernel, (stride, stride), 'VALID', dimension_numbers=('NHWC', 'HWIO', 'NHWC'), precision=lax.Precision.HIGHEST)
    return result[0]

def reference(background, observations, w_station, w_first, w_second, cotangent, station_tile, station_cell):
    channels = background.shape[2]
    station_pre = jnp.dot(observations, w_station, preferred_element_type=jnp.float32)
    embedded = activate(station_pre).astype(jnp.bfloat16)
    target_tile = station_tile[:, 0]
    grid_row = target_tile % N_LAT * LAT_DEV + station_cell // LON_DEV
    grid_col = target_tile // N_LAT * LON_DEV + station_cell % LON_DEV
    grid_index = (grid_row * NLON + grid_col).astype(jnp.int32)
    assimilated = jnp.zeros((NLAT * NLON, channels), jnp.float32).at[grid_index].add(embedded.astype(jnp.float32))
    state = background.astype(jnp.float32).reshape(NLAT * NLON, channels) + assimilated
    state = state.astype(jnp.bfloat16).reshape(NLAT, NLON, channels)
    first_kernel = w_first.astype(jnp.float32)
    second_kernel = w_second.astype(jnp.float32)
    state_wide = state.astype(jnp.float32)
    first_pre = convolve(state_wide, first_kernel, 1)
    hidden = (state_wide + activate(first_pre)).astype(jnp.bfloat16)
    hidden_wide = hidden.astype(jnp.float32)
    encoded = convolve(hidden_wide, second_kernel, 2).astype(jnp.bfloat16)
    second_back = jax.vjp(lambda inner: convolve(inner, second_kernel, 2), hidden_wide)[1]
    hidden_grad = second_back(cotangent.astype(jnp.float32))[0]
    first_grad = activate_back(first_pre, hidden_grad).astype(jnp.bfloat16)
    first_back = jax.vjp(lambda inner: convolve(inner, first_kernel, 1), state_wide)[1]
    state_grad = (hidden_grad + first_back(first_grad.astype(jnp.float32))[0]).astype(jnp.bfloat16)
    station_in = state_grad.reshape(NLAT * NLON, channels)[grid_index]
    station_back = activate_back(station_pre, station_in.astype(jnp.float32)).astype(jnp.bfloat16)
    station_grad = jnp.dot(station_back, w_station.T, preferred_element_type=jnp.float32).astype(jnp.bfloat16)
    weight_grad = jnp.dot(observations.T, station_back, preferred_element_type=jnp.float32)
    weight_grad = weight_grad * (1.0 / math.sqrt(STATIONS))
    return (encoded, station_grad, weight_grad)
```

```python
import math

import jax
import jax.numpy as jnp
from jax import lax
from jax.sharding import PartitionSpec as P

PARITY_TAPS = (((1, 1), (3, 0)), ((0, 2), (2, 1)))


def padded_2(cells, sides, width, closed):
    for axis, dim in sides:
        count = lax.axis_size(axis)
        ends = count if closed else count - 1
        head = lax.slice_in_dim(cells, 0, width, axis=dim)
        tail = lax.slice_in_dim(cells, cells.shape[dim] - width, cells.shape[dim], axis=dim)
        cells = jnp.concatenate(
            [
                lax.ppermute(tail, axis, [(i, (i + 1) % count) for i in range(ends)]),
                cells,
                lax.ppermute(head, axis, [((i + 1) % count, i) for i in range(ends)]),
            ],
            axis=dim,
        )
    return cells


def activate(values):
    return jax.nn.gelu(values, approximate=True)


def activate_back(values, upstream):
    return jax.vjp(activate, values)[1](upstream)[0]


def widen_one(grid_field):
    lon_sides = padded_2(grid_field, (("lon", 1),), 1, True)
    return padded_2(lon_sides, (("lat", 0),), 1, False)


def conv_three(padded, weight):
    height = padded.shape[0] - 2
    breadth = padded.shape[1] - 2
    channels = padded.shape[2]
    kernel_taps = [
        padded[row_shift : row_shift + height, col_shift : col_shift + breadth]
        for row_shift in range(3)
        for col_shift in range(3)
    ]
    patches = jnp.concatenate(kernel_taps, axis=2)
    return jnp.dot(
        patches, weight.reshape(9 * channels, weight.shape[3]), preferred_element_type=jnp.float32
    )


def conv_stride(padded, weight):
    height = padded.shape[0] - 2
    breadth = padded.shape[1] - 2
    channels = padded.shape[2]
    kernel_taps = [
        padded[row_shift : row_shift + height : 2, col_shift : col_shift + breadth : 2]
        for row_shift in range(4)
        for col_shift in range(4)
    ]
    patches = jnp.concatenate(kernel_taps, axis=2)
    return jnp.dot(
        patches, weight.reshape(16 * channels, weight.shape[3]), preferred_element_type=jnp.float32
    )


def conv_three_back(extended, weight):
    height = extended.shape[0] - 2
    breadth = extended.shape[1] - 2
    kernel_taps = [
        extended[2 - row_shift : 2 - row_shift + height, 2 - col_shift : 2 - col_shift + breadth]
        for row_shift in range(3)
        for col_shift in range(3)
    ]
    patches = jnp.stack(kernel_taps, axis=2)
    kernel = weight.reshape(9, weight.shape[2], weight.shape[3])
    return jnp.einsum("hwtk,tck->hwc", patches, kernel, preferred_element_type=jnp.float32)


def conv_stride_back(extended, weight):
    half_height = extended.shape[0] - 2
    half_breadth = extended.shape[1] - 2
    channels = weight.shape[2]
    row_blocks = []
    for row_parity in range(2):
        col_pieces = []
        for col_parity in range(2):
            kernel_taps = []
            kernel_rows = []
            for row_tap, row_start in PARITY_TAPS[row_parity]:
                for col_tap, col_start in PARITY_TAPS[col_parity]:
                    kernel_taps.append(
                        extended[
                            row_start : row_start + half_height,
                            col_start : col_start + half_breadth,
                        ]
                    )
                    kernel_rows.append(weight[row_tap, col_tap])
            patches = jnp.stack(kernel_taps, axis=2)
            kernel = jnp.stack(kernel_rows, axis=0)
            col_pieces.append(
                jnp.einsum("hwtk,tck->hwc", patches, kernel, preferred_element_type=jnp.float32)
            )
        row_blocks.append(jnp.stack(col_pieces, axis=2))
    joined = jnp.stack(row_blocks, axis=1)
    return joined.reshape(2 * half_height, 2 * half_breadth, channels)


def send_out(payload, cell_ids, lon_count, lat_count, capacity):
    feature_width = payload.shape[1]
    got_load, got_cells = (
        lax.all_to_all(
            payload.reshape(lon_count * lat_count, capacity, feature_width),
            ("lon", "lat"),
            split_axis=0,
            concat_axis=0,
            tiled=True,
        ),
        lax.all_to_all(
            cell_ids.reshape(lon_count * lat_count, capacity),
            ("lon", "lat"),
            split_axis=0,
            concat_axis=0,
            tiled=True,
        ),
    )
    return (got_load.reshape(-1, feature_width), got_cells.reshape(-1))


def send_back(reply_rows, lon_count, lat_count, capacity):
    feature_width = reply_rows.shape[1]
    returned = lax.all_to_all(
        reply_rows.reshape(lon_count * lat_count, capacity, feature_width),
        ("lon", "lat"),
        split_axis=0,
        concat_axis=0,
        tiled=True,
    )
    return returned.reshape(-1, feature_width)


def sum_over_devices(term, count):
    rows, width = term.shape
    if rows % count != 0:
        return lax.psum(term, ("lon", "lat"))
    pieces = term.reshape(count, rows // count, width)
    gathered = lax.all_to_all(pieces, ("lon", "lat"), split_axis=0, concat_axis=0, tiled=True)
    own = jnp.sum(gathered, axis=0, keepdims=True)
    spread = jnp.broadcast_to(own, (count, rows // count, width))
    whole = lax.all_to_all(spread, ("lon", "lat"), split_axis=0, concat_axis=0, tiled=True)
    return whole.reshape(rows, width)


def on_device(
    background, observations, w_station, w_first, w_second, cotangent, station_tile, station_cell
):
    lon_count = lax.axis_size("lon")
    lat_count = lax.axis_size("lat")
    tile_count = lon_count * lat_count
    height, breadth, channels = background.shape
    tile_cells = height * breadth
    station_count = observations.shape[0]
    capacity = 2 * station_count // tile_count
    slot_total = tile_count * capacity
    target_tile = station_tile[:, 0]
    matches = (target_tile[:, None] == jnp.arange(tile_count, dtype=jnp.int32)[None, :]).astype(
        jnp.int32
    )
    earlier = jnp.cumsum(matches, axis=0) - matches
    flat_slot = target_tile * capacity + jnp.sum(earlier * matches, axis=1)
    send_cells = jnp.full((slot_total,), -1, jnp.int32).at[flat_slot].set(station_cell)
    station_pre = jnp.dot(observations, w_station, preferred_element_type=jnp.float32)
    payload = activate(station_pre).astype(jnp.bfloat16)
    send_rows = jnp.zeros((slot_total, payload.shape[1]), jnp.bfloat16).at[flat_slot].set(payload)
    got_load, got_cells = send_out(send_rows, send_cells, lon_count, lat_count, capacity)
    cell_match = (jnp.arange(tile_cells, dtype=jnp.int32)[:, None] == got_cells[None, :]).astype(
        jnp.bfloat16
    )
    assimilated = jnp.dot(cell_match, got_load, preferred_element_type=jnp.float32)
    state = background.reshape(tile_cells, channels).astype(jnp.float32) + assimilated
    state = state.astype(jnp.bfloat16).reshape(height, breadth, channels)
    first_pre = conv_three(widen_one(state), w_first)
    hidden = (state.astype(jnp.float32) + activate(first_pre)).astype(jnp.bfloat16)
    encoded = conv_stride(widen_one(hidden), w_second).astype(jnp.bfloat16)
    hidden_grad = conv_stride_back(widen_one(cotangent), w_second)
    first_grad = activate_back(first_pre, hidden_grad).astype(jnp.bfloat16)
    state_grad = hidden_grad + conv_three_back(widen_one(first_grad), w_first)
    state_grad = state_grad.astype(jnp.bfloat16).reshape(tile_cells, channels)
    arrived_grad = lax.dot_general(
        cell_match, state_grad, (((0,), (0,)), ((), ())), preferred_element_type=jnp.float32
    )
    returned = send_back(arrived_grad.astype(jnp.bfloat16), lon_count, lat_count, capacity)
    station_back = activate_back(station_pre, returned[flat_slot].astype(jnp.float32)).astype(
        jnp.bfloat16
    )
    station_grad = lax.dot_general(
        station_back, w_station, (((1,), (1,)), ((), ())), preferred_element_type=jnp.float32
    ).astype(jnp.bfloat16)
    weight_term = lax.dot_general(
        observations, station_back, (((0,), (0,)), ((), ())), preferred_element_type=jnp.float32
    )
    weight_grad = sum_over_devices(weight_term, tile_count)
    weight_grad = weight_grad * (1.0 / math.sqrt(station_count * tile_count))
    return (encoded, station_grad, weight_grad)


def solution(mesh):
    in_specs = (
        P("lat", "lon", None),
        P(("lon", "lat"), None),
        P(),
        P(),
        P(),
        P("lat", "lon", None),
        P(("lon", "lat"), None),
        P(("lon", "lat")),
    )
    out_specs = (P("lat", "lon", None), P(("lon", "lat"), None), P())
    return jax.shard_map(
        on_device, mesh=mesh, in_specs=in_specs, out_specs=out_specs, check_vma=False
    )
```

```python
import math

import jax
import jax.numpy as jnp
from jax import lax
from jax.sharding import PartitionSpec as P

def padded_2(cells, sides, width, closed):
    for axis, dim in sides:
        count = lax.axis_size(axis)
        ends = count if closed else count - 1
        head = lax.slice_in_dim(cells, 0, width, axis=dim)
        tail = lax.slice_in_dim(cells, cells.shape[dim] - width, cells.shape[dim], axis=dim)
        cells = jnp.concatenate(
            [
                lax.ppermute(tail, axis, [(i, (i + 1) % count) for i in range(ends)]),
                cells,
                lax.ppermute(head, axis, [((i + 1) % count, i) for i in range(ends)]),
            ],
            axis=dim,
        )
    return cells


def activate(values):
    return jax.nn.gelu(values, approximate=True)


def activate_back(values, upstream):
    return jax.vjp(activate, values)[1](upstream)[0]


def widen_one(grid_field):
    lon_sides = padded_2(grid_field, (("lon", 1),), 1, True)
    return padded_2(lon_sides, (("lat", 0),), 1, False)


def conv_valid(padded, kernel, stride, dilation, spec):
    result = lax.conv_general_dilated(
        padded[None],
        kernel,
        (stride, stride),
        ((0, 0), (0, 0)),
        lhs_dilation=(dilation, dilation),
        dimension_numbers=("NHWC", spec, "NHWC"),
        preferred_element_type=jnp.float32,
    )
    return result[0]


def conv_three(padded, weight):
    return conv_valid(padded, weight, 1, 1, "HWIO")


def conv_stride(padded, weight):
    return conv_valid(padded, weight, 2, 1, "HWIO")


def conv_three_back(extended, weight):
    return conv_valid(extended, weight[::-1, ::-1], 1, 1, "HWOI")


def conv_stride_back(extended, weight):
    return conv_valid(extended, weight[::-1, ::-1], 1, 2, "HWOI")


def send_out(payload, cell_ids, lon_count, lat_count, capacity):
    feature_width = payload.shape[1]
    got_load, got_cells = (
        lax.all_to_all(
            payload.reshape(lon_count * lat_count, capacity, feature_width),
            ("lon", "lat"),
            split_axis=0,
            concat_axis=0,
            tiled=True,
        ),
        lax.all_to_all(
            cell_ids.reshape(lon_count * lat_count, capacity),
            ("lon", "lat"),
            split_axis=0,
            concat_axis=0,
            tiled=True,
        ),
    )
    return (got_load.reshape(-1, feature_width), got_cells.reshape(-1))


def send_back(reply_rows, lon_count, lat_count, capacity):
    feature_width = reply_rows.shape[1]
    returned = lax.all_to_all(
        reply_rows.reshape(lon_count * lat_count, capacity, feature_width),
        ("lon", "lat"),
        split_axis=0,
        concat_axis=0,
        tiled=True,
    )
    return returned.reshape(-1, feature_width)


def sum_over_devices(term, count):
    rows, width = term.shape
    if rows % count != 0:
        return lax.psum(term, ("lon", "lat"))
    pieces = term.reshape(count, rows // count, width)
    gathered = lax.all_to_all(pieces, ("lon", "lat"), split_axis=0, concat_axis=0, tiled=True)
    own = jnp.sum(gathered, axis=0, keepdims=True)
    spread = jnp.broadcast_to(own, (count, rows // count, width))
    whole = lax.all_to_all(spread, ("lon", "lat"), split_axis=0, concat_axis=0, tiled=True)
    return whole.reshape(rows, width)


def on_device(
    background, observations, w_station, w_first, w_second, cotangent, station_tile, station_cell
):
    lon_count = lax.axis_size("lon")
    lat_count = lax.axis_size("lat")
    tile_count = lon_count * lat_count
    height, breadth, channels = background.shape
    tile_cells = height * breadth
    station_count = observations.shape[0]
    capacity = 2 * station_count // tile_count
    slot_total = tile_count * capacity
    target_tile = station_tile[:, 0]
    matches = (target_tile[:, None] == jnp.arange(tile_count, dtype=jnp.int32)[None, :]).astype(
        jnp.int32
    )
    earlier = jnp.cumsum(matches, axis=0) - matches
    flat_slot = target_tile * capacity + jnp.sum(earlier * matches, axis=1)
    send_cells = jnp.full((slot_total,), -1, jnp.int32).at[flat_slot].set(station_cell)
    station_pre = jnp.dot(observations, w_station, preferred_element_type=jnp.float32)
    payload = activate(station_pre).astype(jnp.bfloat16)
    send_rows = jnp.zeros((slot_total, payload.shape[1]), jnp.bfloat16).at[flat_slot].set(payload)
    got_load, got_cells = send_out(send_rows, send_cells, lon_count, lat_count, capacity)
    cell_match = (jnp.arange(tile_cells, dtype=jnp.int32)[:, None] == got_cells[None, :]).astype(
        jnp.bfloat16
    )
    assimilated = jnp.dot(cell_match, got_load, preferred_element_type=jnp.float32)
    state = background.reshape(tile_cells, channels).astype(jnp.float32) + assimilated
    state = state.astype(jnp.bfloat16).reshape(height, breadth, channels)
    first_pre = conv_three(widen_one(state), w_first)
    hidden = (state.astype(jnp.float32) + activate(first_pre)).astype(jnp.bfloat16)
    encoded = conv_stride(widen_one(hidden), w_second).astype(jnp.bfloat16)
    hidden_grad = conv_stride_back(widen_one(cotangent), w_second)
    first_grad = activate_back(first_pre, hidden_grad).astype(jnp.bfloat16)
    state_grad = hidden_grad + conv_three_back(widen_one(first_grad), w_first)
    state_grad = state_grad.astype(jnp.bfloat16).reshape(tile_cells, channels)
    arrived_grad = lax.dot_general(
        cell_match, state_grad, (((0,), (0,)), ((), ())), preferred_element_type=jnp.float32
    )
    returned = send_back(arrived_grad.astype(jnp.bfloat16), lon_count, lat_count, capacity)
    station_back = activate_back(station_pre, returned[flat_slot].astype(jnp.float32)).astype(
        jnp.bfloat16
    )
    station_grad = lax.dot_general(
        station_back, w_station, (((1,), (1,)), ((), ())), preferred_element_type=jnp.float32
    ).astype(jnp.bfloat16)
    weight_term = lax.dot_general(
        observations, station_back, (((0,), (0,)), ((), ())), preferred_element_type=jnp.float32
    )
    weight_grad = sum_over_devices(weight_term, tile_count)
    weight_grad = weight_grad * (1.0 / math.sqrt(station_count * tile_count))
    return (encoded, station_grad, weight_grad)


def solution(mesh):
    in_specs = (
        P("lat", "lon", None),
        P(("lon", "lat"), None),
        P(),
        P(),
        P(),
        P("lat", "lon", None),
        P(("lon", "lat"), None),
        P(("lon", "lat")),
    )
    out_specs = (P("lat", "lon", None), P(("lon", "lat"), None), P())
    return jax.shard_map(
        on_device, mesh=mesh, in_specs=in_specs, out_specs=out_specs, check_vma=False
    )
```

```python
import math

import jax
import jax.numpy as jnp
from jax import lax
from jax.sharding import PartitionSpec as P

def padded_2(cells, sides, width, closed):
    for axis, dim in sides:
        count = lax.axis_size(axis)
        ends = count if closed else count - 1
        head = lax.slice_in_dim(cells, 0, width, axis=dim)
        tail = lax.slice_in_dim(cells, cells.shape[dim] - width, cells.shape[dim], axis=dim)
        cells = jnp.concatenate(
            [
                lax.ppermute(tail, axis, [(i, (i + 1) % count) for i in range(ends)]),
                cells,
                lax.ppermute(head, axis, [((i + 1) % count, i) for i in range(ends)]),
            ],
            axis=dim,
        )
    return cells


def activate(values):
    return jax.nn.gelu(values, approximate=True)


def activate_back(values, upstream):
    return jax.vjp(activate, values)[1](upstream)[0]


def widen(grid_field, width):
    lon_sides = padded_2(grid_field, (("lon", 1),), width, True)
    return padded_2(lon_sides, (("lat", 0),), width, False)


def inside_rows(field):
    lat_index = lax.axis_index("lat")
    last = lax.axis_size("lat") - 1
    rows = jnp.arange(field.shape[0])[:, None, None]
    outside = ((rows == 0) & (lat_index == 0)) | ((rows == field.shape[0] - 1) & (lat_index == last))
    return jnp.where(outside, jnp.zeros_like(field), field)


def conv_valid(padded, kernel, stride, dilation, spec, rim=0):
    result = lax.conv_general_dilated(
        padded[None],
        kernel,
        (stride, stride),
        ((rim, rim), (rim, rim)),
        lhs_dilation=(dilation, dilation),
        dimension_numbers=("NHWC", spec, "NHWC"),
        preferred_element_type=jnp.float32,
    )
    return result[0]


def conv_three(padded, weight):
    return conv_valid(padded, weight, 1, 1, "HWIO")


def conv_stride(padded, weight):
    return conv_valid(padded, weight, 2, 1, "HWIO")


def conv_three_back(extended, weight):
    return conv_valid(extended, weight[::-1, ::-1], 1, 1, "HWOI")


def conv_stride_back(extended, weight):
    return conv_valid(extended, weight[::-1, ::-1], 1, 2, "HWOI", 1)


def send_out(payload, cell_ids, lon_count, lat_count, capacity):
    feature_width = payload.shape[1]
    got_load, got_cells = (
        lax.all_to_all(
            payload.reshape(lon_count * lat_count, capacity, feature_width),
            ("lon", "lat"),
            split_axis=0,
            concat_axis=0,
            tiled=True,
        ),
        lax.all_to_all(
            cell_ids.reshape(lon_count * lat_count, capacity),
            ("lon", "lat"),
            split_axis=0,
            concat_axis=0,
            tiled=True,
        ),
    )
    return (got_load.reshape(-1, feature_width), got_cells.reshape(-1))


def send_back(reply_rows, lon_count, lat_count, capacity):
    feature_width = reply_rows.shape[1]
    returned = lax.all_to_all(
        reply_rows.reshape(lon_count * lat_count, capacity, feature_width),
        ("lon", "lat"),
        split_axis=0,
        concat_axis=0,
        tiled=True,
    )
    return returned.reshape(-1, feature_width)


def sum_over_devices(term, count):
    rows, width = term.shape
    if rows % count != 0:
        return lax.psum(term, ("lon", "lat"))
    pieces = term.reshape(count, rows // count, width)
    gathered = lax.all_to_all(pieces, ("lon", "lat"), split_axis=0, concat_axis=0, tiled=True)
    own = jnp.sum(gathered, axis=0, keepdims=True)
    spread = jnp.broadcast_to(own, (count, rows // count, width))
    whole = lax.all_to_all(spread, ("lon", "lat"), split_axis=0, concat_axis=0, tiled=True)
    return whole.reshape(rows, width)


def on_device(
    background, observations, w_station, w_first, w_second, cotangent, station_tile, station_cell
):
    lon_count = lax.axis_size("lon")
    lat_count = lax.axis_size("lat")
    tile_count = lon_count * lat_count
    height, breadth, channels = background.shape
    tile_cells = height * breadth
    station_count = observations.shape[0]
    capacity = 2 * station_count // tile_count
    slot_total = tile_count * capacity
    target_tile = station_tile[:, 0]
    matches = (target_tile[:, None] == jnp.arange(tile_count, dtype=jnp.int32)[None, :]).astype(
        jnp.int32
    )
    earlier = jnp.cumsum(matches, axis=0) - matches
    flat_slot = target_tile * capacity + jnp.sum(earlier * matches, axis=1)
    send_cells = jnp.full((slot_total,), -1, jnp.int32).at[flat_slot].set(station_cell)
    station_pre = jnp.dot(observations, w_station, preferred_element_type=jnp.float32)
    payload = activate(station_pre).astype(jnp.bfloat16)
    send_rows = jnp.zeros((slot_total, payload.shape[1]), jnp.bfloat16).at[flat_slot].set(payload)
    got_load, got_cells = send_out(send_rows, send_cells, lon_count, lat_count, capacity)
    cell_match = (jnp.arange(tile_cells, dtype=jnp.int32)[:, None] == got_cells[None, :]).astype(
        jnp.bfloat16
    )
    assimilated = jnp.dot(cell_match, got_load, preferred_element_type=jnp.float32)
    state = background.reshape(tile_cells, channels).astype(jnp.float32) + assimilated
    state = state.astype(jnp.bfloat16).reshape(height, breadth, channels)
    state_rim = widen(state, 2)
    cotangent_rim = widen(cotangent, 1)
    first_pre = conv_three(state_rim, w_first)
    state_near = state_rim[1:-1, 1:-1].astype(jnp.float32)
    hidden = inside_rows((state_near + activate(first_pre)).astype(jnp.bfloat16))
    encoded = conv_stride(hidden, w_second).astype(jnp.bfloat16)
    hidden_grad = conv_stride_back(cotangent_rim, w_second)
    first_grad = inside_rows(activate_back(first_pre, hidden_grad).astype(jnp.bfloat16))
    state_grad = hidden_grad[1:-1, 1:-1] + conv_three_back(first_grad, w_first)
    state_grad = state_grad.astype(jnp.bfloat16).reshape(tile_cells, channels)
    arrived_grad = lax.dot_general(
        cell_match, state_grad, (((0,), (0,)), ((), ())), preferred_element_type=jnp.float32
    )
    returned = send_back(arrived_grad.astype(jnp.bfloat16), lon_count, lat_count, capacity)
    station_back = activate_back(station_pre, returned[flat_slot].astype(jnp.float32)).astype(
        jnp.bfloat16
    )
    station_grad = lax.dot_general(
        station_back, w_station, (((1,), (1,)), ((), ())), preferred_element_type=jnp.float32
    ).astype(jnp.bfloat16)
    weight_term = lax.dot_general(
        observations, station_back, (((0,), (0,)), ((), ())), preferred_element_type=jnp.float32
    )
    weight_grad = sum_over_devices(weight_term, tile_count)
    weight_grad = weight_grad * (1.0 / math.sqrt(station_count * tile_count))
    return (encoded, station_grad, weight_grad)


def solution(mesh):
    in_specs = (
        P("lat", "lon", None),
        P(("lon", "lat"), None),
        P(),
        P(),
        P(),
        P("lat", "lon", None),
        P(("lon", "lat"), None),
        P(("lon", "lat")),
    )
    out_specs = (P("lat", "lon", None), P(("lon", "lat"), None), P())
    return jax.shard_map(
        on_device, mesh=mesh, in_specs=in_specs, out_specs=out_specs, check_vma=False
    )
```

```python
import math

import jax
import jax.numpy as jnp
from jax import lax
from jax.sharding import PartitionSpec as P

def padded_2(cells, sides, width, closed):
    for axis, dim in sides:
        count = lax.axis_size(axis)
        ends = count if closed else count - 1
        head = lax.slice_in_dim(cells, 0, width, axis=dim)
        tail = lax.slice_in_dim(cells, cells.shape[dim] - width, cells.shape[dim], axis=dim)
        cells = jnp.concatenate(
            [
                lax.ppermute(tail, axis, [(i, (i + 1) % count) for i in range(ends)]),
                cells,
                lax.ppermute(head, axis, [((i + 1) % count, i) for i in range(ends)]),
            ],
            axis=dim,
        )
    return cells


def activate(values):
    return jax.nn.gelu(values, approximate=True)


def activate_back(values, upstream):
    return jax.vjp(activate, values)[1](upstream)[0]


def widen(grid_field, width):
    lon_sides = padded_2(grid_field, (("lon", 1),), width, True)
    return padded_2(lon_sides, (("lat", 0),), width, False)


def inside_rows(field):
    lat_index = lax.axis_index("lat")
    last = lax.axis_size("lat") - 1
    rows = jnp.arange(field.shape[0])[:, None, None]
    outside = ((rows == 0) & (lat_index == 0)) | ((rows == field.shape[0] - 1) & (lat_index == last))
    return jnp.where(outside, jnp.zeros_like(field), field)


def conv_valid(padded, kernel, stride, dilation, spec, rim=0):
    result = lax.conv_general_dilated(
        padded[None],
        kernel,
        (stride, stride),
        ((rim, rim), (rim, rim)),
        lhs_dilation=(dilation, dilation),
        dimension_numbers=("NHWC", spec, "NHWC"),
        preferred_element_type=jnp.float32,
    )
    return result[0]


def conv_three(padded, weight):
    return conv_valid(padded, weight, 1, 1, "HWIO")


def conv_stride(padded, weight):
    return conv_valid(padded, weight, 2, 1, "HWIO")


def conv_three_back(extended, weight):
    return conv_valid(extended, weight[::-1, ::-1], 1, 1, "HWOI")


def conv_stride_back(extended, weight):
    return conv_valid(extended, weight[::-1, ::-1], 1, 2, "HWOI", 1)


def send_out(payload, cell_ids, lon_count, lat_count, capacity):
    feature_width = payload.shape[1]
    got_load, got_cells = (
        lax.all_to_all(
            payload.reshape(lon_count * lat_count, capacity, feature_width),
            ("lon", "lat"),
            split_axis=0,
            concat_axis=0,
            tiled=True,
        ),
        lax.all_to_all(
            cell_ids.reshape(lon_count * lat_count, capacity),
            ("lon", "lat"),
            split_axis=0,
            concat_axis=0,
            tiled=True,
        ),
    )
    return (got_load.reshape(-1, feature_width), got_cells.reshape(-1))


def send_back(reply_rows, lon_count, lat_count, capacity):
    feature_width = reply_rows.shape[1]
    returned = lax.all_to_all(
        reply_rows.reshape(lon_count * lat_count, capacity, feature_width),
        ("lon", "lat"),
        split_axis=0,
        concat_axis=0,
        tiled=True,
    )
    return returned.reshape(-1, feature_width)


def sum_over_devices(term, count):
    rows, width = term.shape
    if rows % count != 0:
        return lax.psum(term, ("lon", "lat"))
    pieces = term.reshape(count, rows // count, width)
    gathered = lax.all_to_all(pieces, ("lon", "lat"), split_axis=0, concat_axis=0, tiled=True)
    own = jnp.sum(gathered, axis=0, keepdims=True)
    spread = jnp.broadcast_to(own, (count, rows // count, width))
    whole = lax.all_to_all(spread, ("lon", "lat"), split_axis=0, concat_axis=0, tiled=True)
    return whole.reshape(rows, width)


def on_device(
    background, observations, w_station, w_first, w_second, cotangent, station_tile, station_cell
):
    lon_count = lax.axis_size("lon")
    lat_count = lax.axis_size("lat")
    tile_count = lon_count * lat_count
    height, breadth, channels = background.shape
    tile_cells = height * breadth
    station_count = observations.shape[0]
    capacity = 2 * station_count // tile_count
    slot_total = tile_count * capacity
    target_tile = station_tile[:, 0]
    matches = (target_tile[:, None] == jnp.arange(tile_count, dtype=jnp.int32)[None, :]).astype(
        jnp.int32
    )
    earlier = jnp.cumsum(matches, axis=0) - matches
    flat_slot = target_tile * capacity + jnp.sum(earlier * matches, axis=1)
    send_cells = jnp.full((slot_total,), -1, jnp.int32).at[flat_slot].set(station_cell)
    station_pre = jnp.dot(observations, w_station, preferred_element_type=jnp.float32)
    payload = activate(station_pre).astype(jnp.bfloat16)
    send_rows = jnp.zeros((slot_total, payload.shape[1]), jnp.bfloat16).at[flat_slot].set(payload)
    got_load, got_cells = send_out(send_rows, send_cells, lon_count, lat_count, capacity)
    cell_match = (jnp.arange(tile_cells, dtype=jnp.int32)[:, None] == got_cells[None, :]).astype(
        jnp.bfloat16
    )
    assimilated = jnp.dot(cell_match, got_load, preferred_element_type=jnp.float32)
    state = background.reshape(tile_cells, channels).astype(jnp.float32) + assimilated
    state = state.astype(jnp.bfloat16).reshape(height, breadth, channels)
    state_rim = widen(state, 2)
    cotangent_rim = widen(cotangent, 1)
    first_pre = conv_three(state_rim, w_first)
    state_near = state_rim[1:-1, 1:-1].astype(jnp.float32)
    hidden = inside_rows((state_near + activate(first_pre)).astype(jnp.bfloat16))
    encoded = conv_stride(hidden, w_second).astype(jnp.bfloat16)
    hidden_grad = conv_stride_back(cotangent_rim, w_second)
    first_pre_again = lax.optimization_barrier(first_pre)
    first_grad = inside_rows(activate_back(first_pre_again, hidden_grad).astype(jnp.bfloat16))
    state_grad = hidden_grad[1:-1, 1:-1] + conv_three_back(first_grad, w_first)
    state_grad = state_grad.astype(jnp.bfloat16).reshape(tile_cells, channels)
    arrived_grad = lax.dot_general(
        cell_match, state_grad, (((0,), (0,)), ((), ())), preferred_element_type=jnp.float32
    )
    returned = send_back(arrived_grad.astype(jnp.bfloat16), lon_count, lat_count, capacity)
    station_back = activate_back(station_pre, returned[flat_slot].astype(jnp.float32)).astype(
        jnp.bfloat16
    )
    station_grad = lax.dot_general(
        station_back, w_station, (((1,), (1,)), ((), ())), preferred_element_type=jnp.float32
    ).astype(jnp.bfloat16)
    weight_term = lax.dot_general(
        observations, station_back, (((0,), (0,)), ((), ())), preferred_element_type=jnp.float32
    )
    weight_grad = sum_over_devices(weight_term, tile_count)
    weight_grad = weight_grad * (1.0 / math.sqrt(station_count * tile_count))
    return (encoded, station_grad, weight_grad)


def solution(mesh):
    in_specs = (
        P("lat", "lon", None),
        P(("lon", "lat"), None),
        P(),
        P(),
        P(),
        P("lat", "lon", None),
        P(("lon", "lat"), None),
        P(("lon", "lat")),
    )
    out_specs = (P("lat", "lon", None), P(("lon", "lat"), None), P())
    return jax.shard_map(
        on_device, mesh=mesh, in_specs=in_specs, out_specs=out_specs, check_vma=False
    )
```

```python
import math

import jax
import jax.numpy as jnp
from jax import lax
from jax.sharding import PartitionSpec as P

def padded_2(cells, sides, width, closed):
    for axis, dim in sides:
        count = lax.axis_size(axis)
        ends = count if closed else count - 1
        head = lax.slice_in_dim(cells, 0, width, axis=dim)
        tail = lax.slice_in_dim(cells, cells.shape[dim] - width, cells.shape[dim], axis=dim)
        cells = jnp.concatenate(
            [
                lax.ppermute(tail, axis, [(i, (i + 1) % count) for i in range(ends)]),
                cells,
                lax.ppermute(head, axis, [((i + 1) % count, i) for i in range(ends)]),
            ],
            axis=dim,
        )
    return cells


def activate(values):
    return jax.nn.gelu(values, approximate=True)


def activate_back(values, upstream):
    return jax.vjp(activate, values)[1](upstream)[0]


def widen(grid_field, width):
    lon_sides = padded_2(grid_field, (("lon", 1),), width, True)
    return padded_2(lon_sides, (("lat", 0),), width, False)


def inside_rows(field):
    lat_index = lax.axis_index("lat")
    last = lax.axis_size("lat") - 1
    rows = jnp.arange(field.shape[0])[:, None, None]
    outside = ((rows == 0) & (lat_index == 0)) | ((rows == field.shape[0] - 1) & (lat_index == last))
    return jnp.where(outside, jnp.zeros_like(field), field)


def conv_valid(padded, kernel, stride, dilation, spec, rim=0):
    result = lax.conv_general_dilated(
        padded[None],
        kernel,
        (stride, stride),
        ((rim, rim), (rim, rim)),
        lhs_dilation=(dilation, dilation),
        dimension_numbers=("NHWC", spec, "NHWC"),
        preferred_element_type=jnp.float32,
    )
    return result[0]


def conv_three(padded, weight):
    return conv_valid(padded, weight, 1, 1, "HWIO")


def conv_stride(padded, weight):
    return conv_valid(padded, weight, 2, 1, "HWIO")


def conv_three_back(extended, weight):
    return conv_valid(extended, weight[::-1, ::-1], 1, 1, "HWOI")


def conv_stride_back(extended, weight):
    return conv_valid(extended, weight[::-1, ::-1], 1, 2, "HWOI", 1)


def send_out(payload, cell_ids, lon_count, lat_count, capacity):
    feature_width = payload.shape[1]
    got_load, got_cells = (
        lax.all_to_all(
            payload.reshape(lon_count * lat_count, capacity, feature_width),
            ("lon", "lat"),
            split_axis=0,
            concat_axis=0,
            tiled=True,
        ),
        lax.all_to_all(
            cell_ids.reshape(lon_count * lat_count, capacity),
            ("lon", "lat"),
            split_axis=0,
            concat_axis=0,
            tiled=True,
        ),
    )
    return (got_load.reshape(-1, feature_width), got_cells.reshape(-1))


def send_back(reply_rows, lon_count, lat_count, capacity):
    feature_width = reply_rows.shape[1]
    returned = lax.all_to_all(
        reply_rows.reshape(lon_count * lat_count, capacity, feature_width),
        ("lon", "lat"),
        split_axis=0,
        concat_axis=0,
        tiled=True,
    )
    return returned.reshape(-1, feature_width)


def sum_over_devices(term, count):
    rows, width = term.shape
    if rows % count != 0:
        return lax.psum(term, ("lon", "lat"))
    pieces = term.reshape(count, rows // count, width)
    gathered = lax.all_to_all(pieces, ("lon", "lat"), split_axis=0, concat_axis=0, tiled=True)
    own = jnp.sum(gathered, axis=0, keepdims=True)
    spread = jnp.broadcast_to(own, (count, rows // count, width))
    whole = lax.all_to_all(spread, ("lon", "lat"), split_axis=0, concat_axis=0, tiled=True)
    return whole.reshape(rows, width)


def on_device(
    background, observations, w_station, w_first, w_second, cotangent, station_tile, station_cell
):
    lon_count = lax.axis_size("lon")
    lat_count = lax.axis_size("lat")
    tile_count = lon_count * lat_count
    height, breadth, channels = background.shape
    tile_cells = height * breadth
    station_count = observations.shape[0]
    capacity = 2 * station_count // tile_count
    slot_total = tile_count * capacity
    target_tile = station_tile[:, 0]
    matches = (target_tile[:, None] == jnp.arange(tile_count, dtype=jnp.int32)[None, :]).astype(
        jnp.bfloat16
    )
    order = jnp.arange(station_count, dtype=jnp.int32)
    before = (order[:, None] > order[None, :]).astype(jnp.bfloat16)
    earlier = jnp.dot(before, matches, preferred_element_type=jnp.float32)
    rank = jnp.sum(earlier * matches.astype(jnp.float32), axis=1).astype(jnp.int32)
    flat_slot = target_tile * capacity + rank
    slot_hit = jnp.arange(slot_total, dtype=jnp.int32)[:, None] == flat_slot[None, :]
    slot_pick = slot_hit.astype(jnp.bfloat16)
    send_cells = jnp.sum(jnp.where(slot_hit, station_cell[None, :] + 1, 0), axis=1) - 1
    send_rows = jnp.dot(slot_pick, observations, preferred_element_type=jnp.float32).astype(
        jnp.bfloat16
    )
    got_obs, got_cells = send_out(send_rows, send_cells, lon_count, lat_count, capacity)
    slot_pre = jnp.dot(got_obs, w_station, preferred_element_type=jnp.float32)
    slot_embedded = activate(slot_pre).astype(jnp.bfloat16)
    cell_match = (jnp.arange(tile_cells, dtype=jnp.int32)[:, None] == got_cells[None, :]).astype(
        jnp.bfloat16
    )
    assimilated = jnp.dot(cell_match, slot_embedded, preferred_element_type=jnp.float32)
    state = background.reshape(tile_cells, channels).astype(jnp.float32) + assimilated
    state = state.astype(jnp.bfloat16).reshape(height, breadth, channels)
    state_rim = widen(state, 2)
    cotangent_rim = widen(cotangent, 1)
    first_pre = conv_three(state_rim, w_first)
    state_near = state_rim[1:-1, 1:-1].astype(jnp.float32)
    hidden = inside_rows((state_near + activate(first_pre)).astype(jnp.bfloat16))
    encoded = conv_stride(hidden, w_second).astype(jnp.bfloat16)
    hidden_grad = conv_stride_back(cotangent_rim, w_second)
    first_pre_again = lax.optimization_barrier(first_pre)
    first_grad = inside_rows(activate_back(first_pre_again, hidden_grad).astype(jnp.bfloat16))
    state_grad = hidden_grad[1:-1, 1:-1] + conv_three_back(first_grad, w_first)
    state_grad = state_grad.astype(jnp.bfloat16).reshape(tile_cells, channels)
    arrived_grad = lax.dot_general(
        cell_match, state_grad, (((0,), (0,)), ((), ())), preferred_element_type=jnp.float32
    )
    slot_back = activate_back(slot_pre, arrived_grad).astype(jnp.bfloat16)
    slot_grad = lax.dot_general(
        slot_back, w_station, (((1,), (1,)), ((), ())), preferred_element_type=jnp.float32
    ).astype(jnp.bfloat16)
    weight_term = lax.dot_general(
        got_obs, slot_back, (((0,), (0,)), ((), ())), preferred_element_type=jnp.float32
    )
    returned = send_back(slot_grad, lon_count, lat_count, capacity)
    station_grad = lax.dot_general(
        slot_pick, returned, (((0,), (0,)), ((), ())), preferred_element_type=jnp.float32
    ).astype(jnp.bfloat16)
    weight_grad = sum_over_devices(weight_term, tile_count)
    weight_grad = weight_grad * (1.0 / math.sqrt(station_count * tile_count))
    return (encoded, station_grad, weight_grad)


def solution(mesh):
    in_specs = (
        P("lat", "lon", None),
        P(("lon", "lat"), None),
        P(),
        P(),
        P(),
        P("lat", "lon", None),
        P(("lon", "lat"), None),
        P(("lon", "lat")),
    )
    out_specs = (P("lat", "lon", None), P(("lon", "lat"), None), P())
    return jax.shard_map(
        on_device, mesh=mesh, in_specs=in_specs, out_specs=out_specs, check_vma=False
    )
```

```python
import math

import jax
import jax.numpy as jnp
from jax import lax
from jax.sharding import PartitionSpec as P

def activate(values):
    return jax.nn.gelu(values, approximate=True)


def activate_back(values, upstream):
    return jax.vjp(activate, values)[1](upstream)[0]


def exchange(fields, axis, dim, closed):
    count = lax.axis_size(axis)
    ends = count if closed else count - 1
    heads = [lax.slice_in_dim(f, 0, w, axis=dim) for f, w in fields]
    tails = [lax.slice_in_dim(f, f.shape[dim] - w, f.shape[dim], axis=dim) for f, w in fields]

    def pack(parts):
        return jnp.concatenate([p.reshape(-1, p.shape[-1]) for p in parts], axis=0)

    def unpack(packed, like):
        pieces, at = [], 0
        for p in like:
            rows = p.size // p.shape[-1]
            pieces.append(packed[at : at + rows].reshape(p.shape))
            at += rows
        return pieces

    got_tails = unpack(
        lax.ppermute(pack(tails), axis, [(i, (i + 1) % count) for i in range(ends)]), tails
    )
    got_heads = unpack(
        lax.ppermute(pack(heads), axis, [((i + 1) % count, i) for i in range(ends)]), heads
    )
    return [
        jnp.concatenate([t, f, h], axis=dim)
        for (f, _), t, h in zip(fields, got_tails, got_heads)
    ]


def widen_both(state, cotangent):
    state_lon, cotangent_lon = exchange([(state, 2), (cotangent, 1)], "lon", 1, True)
    return exchange([(state_lon, 2), (cotangent_lon, 1)], "lat", 0, False)


def inside_rows(field):
    lat_index = lax.axis_index("lat")
    last = lax.axis_size("lat") - 1
    rows = jnp.arange(field.shape[0])[:, None, None]
    outside = ((rows == 0) & (lat_index == 0)) | ((rows == field.shape[0] - 1) & (lat_index == last))
    return jnp.where(outside, jnp.zeros_like(field), field)


def conv_valid(padded, kernel, stride, dilation, spec, rim=0):
    result = lax.conv_general_dilated(
        padded[None],
        kernel,
        (stride, stride),
        ((rim, rim), (rim, rim)),
        lhs_dilation=(dilation, dilation),
        dimension_numbers=("NHWC", spec, "NHWC"),
        preferred_element_type=jnp.float32,
    )
    return result[0]


def conv_three(padded, weight):
    return conv_valid(padded, weight, 1, 1, "HWIO")


def conv_stride(padded, weight):
    return conv_valid(padded, weight, 2, 1, "HWIO")


def conv_three_back(extended, weight):
    return conv_valid(extended, weight[::-1, ::-1], 1, 1, "HWOI")


def conv_stride_back(extended, weight):
    return conv_valid(extended, weight[::-1, ::-1], 1, 2, "HWOI", 1)


def send_out(payload, cell_ids, lon_count, lat_count, capacity):
    feature_width = payload.shape[1]
    got_load, got_cells = (
        lax.all_to_all(
            payload.reshape(lon_count * lat_count, capacity, feature_width),
            ("lon", "lat"),
            split_axis=0,
            concat_axis=0,
            tiled=True,
        ),
        lax.all_to_all(
            cell_ids.reshape(lon_count * lat_count, capacity),
            ("lon", "lat"),
            split_axis=0,
            concat_axis=0,
            tiled=True,
        ),
    )
    return (got_load.reshape(-1, feature_width), got_cells.reshape(-1))


def send_back(reply_rows, lon_count, lat_count, capacity):
    feature_width = reply_rows.shape[1]
    returned = lax.all_to_all(
        reply_rows.reshape(lon_count * lat_count, capacity, feature_width),
        ("lon", "lat"),
        split_axis=0,
        concat_axis=0,
        tiled=True,
    )
    return returned.reshape(-1, feature_width)


def sum_over_devices(term, count):
    rows, width = term.shape
    if rows % count != 0:
        return lax.psum(term, ("lon", "lat"))
    pieces = term.reshape(count, rows // count, width)
    gathered = lax.all_to_all(pieces, ("lon", "lat"), split_axis=0, concat_axis=0, tiled=True)
    own = jnp.sum(gathered, axis=0, keepdims=True)
    spread = jnp.broadcast_to(own, (count, rows // count, width))
    whole = lax.all_to_all(spread, ("lon", "lat"), split_axis=0, concat_axis=0, tiled=True)
    return whole.reshape(rows, width)


def on_device(
    background, observations, w_station, w_first, w_second, cotangent, station_tile, station_cell
):
    lon_count = lax.axis_size("lon")
    lat_count = lax.axis_size("lat")
    tile_count = lon_count * lat_count
    height, breadth, channels = background.shape
    tile_cells = height * breadth
    station_count = observations.shape[0]
    capacity = 2 * station_count // tile_count
    slot_total = tile_count * capacity
    target_tile = station_tile[:, 0]
    matches = (target_tile[:, None] == jnp.arange(tile_count, dtype=jnp.int32)[None, :]).astype(
        jnp.bfloat16
    )
    order = jnp.arange(station_count, dtype=jnp.int32)
    before = (order[:, None] > order[None, :]).astype(jnp.bfloat16)
    earlier = jnp.dot(before, matches, preferred_element_type=jnp.float32)
    rank = jnp.sum(earlier * matches.astype(jnp.float32), axis=1).astype(jnp.int32)
    flat_slot = target_tile * capacity + rank
    slot_hit = jnp.arange(slot_total, dtype=jnp.int32)[:, None] == flat_slot[None, :]
    slot_pick = slot_hit.astype(jnp.bfloat16)
    send_cells = jnp.sum(jnp.where(slot_hit, station_cell[None, :] + 1, 0), axis=1) - 1
    send_rows = jnp.dot(slot_pick, observations, preferred_element_type=jnp.float32).astype(
        jnp.bfloat16
    )
    got_obs, got_cells = send_out(send_rows, send_cells, lon_count, lat_count, capacity)
    slot_pre = jnp.dot(got_obs, w_station, preferred_element_type=jnp.float32)
    slot_embedded = activate(slot_pre).astype(jnp.bfloat16)
    cell_match = (jnp.arange(tile_cells, dtype=jnp.int32)[:, None] == got_cells[None, :]).astype(
        jnp.bfloat16
    )
    assimilated = jnp.dot(cell_match, slot_embedded, preferred_element_type=jnp.float32)
    state = background.reshape(tile_cells, channels).astype(jnp.float32) + assimilated
    state = state.astype(jnp.bfloat16).reshape(height, breadth, channels)
    state_rim, cotangent_rim = widen_both(state, cotangent)
    first_pre = conv_three(state_rim, w_first)
    state_near = state_rim[1:-1, 1:-1].astype(jnp.float32)
    hidden = inside_rows((state_near + activate(first_pre)).astype(jnp.bfloat16))
    encoded = conv_stride(hidden, w_second).astype(jnp.bfloat16)
    hidden_grad = conv_stride_back(cotangent_rim, w_second)
    first_pre_again = lax.optimization_barrier(first_pre)
    first_grad = inside_rows(activate_back(first_pre_again, hidden_grad).astype(jnp.bfloat16))
    state_grad = hidden_grad[1:-1, 1:-1] + conv_three_back(first_grad, w_first)
    state_grad = state_grad.astype(jnp.bfloat16).reshape(tile_cells, channels)
    arrived_grad = lax.dot_general(
        cell_match, state_grad, (((0,), (0,)), ((), ())), preferred_element_type=jnp.float32
    )
    slot_back = activate_back(slot_pre, arrived_grad).astype(jnp.bfloat16)
    slot_grad = lax.dot_general(
        slot_back, w_station, (((1,), (1,)), ((), ())), preferred_element_type=jnp.float32
    ).astype(jnp.bfloat16)
    weight_term = lax.dot_general(
        got_obs, slot_back, (((0,), (0,)), ((), ())), preferred_element_type=jnp.float32
    )
    returned = send_back(slot_grad, lon_count, lat_count, capacity)
    station_grad = lax.dot_general(
        slot_pick, returned, (((0,), (0,)), ((), ())), preferred_element_type=jnp.float32
    ).astype(jnp.bfloat16)
    weight_grad = sum_over_devices(weight_term, tile_count)
    weight_grad = weight_grad * (1.0 / math.sqrt(station_count * tile_count))
    return (encoded, station_grad, weight_grad)


def solution(mesh):
    in_specs = (
        P("lat", "lon", None),
        P(("lon", "lat"), None),
        P(),
        P(),
        P(),
        P("lat", "lon", None),
        P(("lon", "lat"), None),
        P(("lon", "lat")),
    )
    out_specs = (P("lat", "lon", None), P(("lon", "lat"), None), P())
    return jax.shard_map(
        on_device, mesh=mesh, in_specs=in_specs, out_specs=out_specs, check_vma=False
    )
```

```python
import math

import jax
import jax.numpy as jnp
from jax import lax
from jax.sharding import PartitionSpec as P

def padded_2(cells, sides, width, closed):
    for axis, dim in sides:
        count = lax.axis_size(axis)
        ends = count if closed else count - 1
        head = lax.slice_in_dim(cells, 0, width, axis=dim)
        tail = lax.slice_in_dim(cells, cells.shape[dim] - width, cells.shape[dim], axis=dim)
        cells = jnp.concatenate(
            [
                lax.ppermute(tail, axis, [(i, (i + 1) % count) for i in range(ends)]),
                cells,
                lax.ppermute(head, axis, [((i + 1) % count, i) for i in range(ends)]),
            ],
            axis=dim,
        )
    return cells


def activate(values):
    return jax.nn.gelu(values, approximate=True)


def activate_back(values, upstream):
    return jax.vjp(activate, values)[1](upstream)[0]


def widen(grid_field, width):
    lon_sides = padded_2(grid_field, (("lon", 1),), width, True)
    return padded_2(lon_sides, (("lat", 0),), width, False)


def inside_rows(field):
    lat_index = lax.axis_index("lat")
    last = lax.axis_size("lat") - 1
    rows = jnp.arange(field.shape[0])[:, None, None]
    outside = ((rows == 0) & (lat_index == 0)) | ((rows == field.shape[0] - 1) & (lat_index == last))
    return jnp.where(outside, jnp.zeros_like(field), field)


def conv_valid(padded, kernel, stride, dilation, spec, rim=0):
    result = lax.conv_general_dilated(
        padded[None],
        kernel,
        (stride, stride),
        ((rim, rim), (rim, rim)),
        lhs_dilation=(dilation, dilation),
        dimension_numbers=("NHWC", spec, "NHWC"),
        preferred_element_type=jnp.float32,
    )
    return result[0]


def conv_three(padded, weight):
    return conv_valid(padded, weight, 1, 1, "HWIO")


def conv_stride(padded, weight):
    return conv_valid(padded, weight, 2, 1, "HWIO")


def conv_three_back(extended, weight):
    return conv_valid(extended, weight[::-1, ::-1], 1, 1, "HWOI")


def conv_stride_back(extended, weight):
    return conv_valid(extended, weight[::-1, ::-1], 1, 2, "HWOI", 1)


def send_out(payload, cell_ids, lon_count, lat_count, capacity):
    feature_width = payload.shape[1]
    tile_count = lon_count * lat_count
    shifted = cell_ids.reshape(tile_count, capacity) + 1
    high = (shifted // 64).astype(payload.dtype)
    low = (shifted % 64).astype(payload.dtype)
    packed = jnp.concatenate(
        [payload.reshape(tile_count, capacity * feature_width), high, low], axis=1
    )
    got = lax.all_to_all(packed, ("lon", "lat"), split_axis=0, concat_axis=0, tiled=True)
    got_load = got[:, : capacity * feature_width].reshape(-1, feature_width)
    got_high = got[:, capacity * feature_width : capacity * (feature_width + 1)]
    got_low = got[:, capacity * (feature_width + 1) :]
    got_cells = got_high.astype(jnp.int32) * 64 + got_low.astype(jnp.int32) - 1
    return (got_load, got_cells.reshape(-1))


def send_back(reply_rows, lon_count, lat_count, capacity):
    feature_width = reply_rows.shape[1]
    returned = lax.all_to_all(
        reply_rows.reshape(lon_count * lat_count, capacity, feature_width),
        ("lon", "lat"),
        split_axis=0,
        concat_axis=0,
        tiled=True,
    )
    return returned.reshape(-1, feature_width)


def sum_over_devices(term, count):
    rows, width = term.shape
    if rows % count != 0:
        return lax.psum(term, ("lon", "lat"))
    pieces = term.reshape(count, rows // count, width)
    gathered = lax.all_to_all(pieces, ("lon", "lat"), split_axis=0, concat_axis=0, tiled=True)
    own = jnp.sum(gathered, axis=0, keepdims=True)
    spread = jnp.broadcast_to(own, (count, rows // count, width))
    whole = lax.all_to_all(spread, ("lon", "lat"), split_axis=0, concat_axis=0, tiled=True)
    return whole.reshape(rows, width)


def on_device(
    background, observations, w_station, w_first, w_second, cotangent, station_tile, station_cell
):
    lon_count = lax.axis_size("lon")
    lat_count = lax.axis_size("lat")
    tile_count = lon_count * lat_count
    height, breadth, channels = background.shape
    tile_cells = height * breadth
    station_count = observations.shape[0]
    capacity = 2 * station_count // tile_count
    slot_total = tile_count * capacity
    target_tile = station_tile[:, 0]
    matches = (target_tile[:, None] == jnp.arange(tile_count, dtype=jnp.int32)[None, :]).astype(
        jnp.bfloat16
    )
    order = jnp.arange(station_count, dtype=jnp.int32)
    before = (order[:, None] > order[None, :]).astype(jnp.bfloat16)
    earlier = jnp.dot(before, matches, preferred_element_type=jnp.float32)
    rank = jnp.sum(earlier * matches.astype(jnp.float32), axis=1).astype(jnp.int32)
    flat_slot = target_tile * capacity + rank
    slot_hit = jnp.arange(slot_total, dtype=jnp.int32)[:, None] == flat_slot[None, :]
    slot_pick = slot_hit.astype(jnp.bfloat16)
    send_cells = jnp.sum(jnp.where(slot_hit, station_cell[None, :] + 1, 0), axis=1) - 1
    send_rows = jnp.dot(slot_pick, observations, preferred_element_type=jnp.float32).astype(
        jnp.bfloat16
    )
    got_obs, got_cells = send_out(send_rows, send_cells, lon_count, lat_count, capacity)
    slot_pre = jnp.dot(got_obs, w_station, preferred_element_type=jnp.float32)
    slot_embedded = activate(slot_pre).astype(jnp.bfloat16)
    cell_match = (jnp.arange(tile_cells, dtype=jnp.int32)[:, None] == got_cells[None, :]).astype(
        jnp.bfloat16
    )
    assimilated = jnp.dot(cell_match, slot_embedded, preferred_element_type=jnp.float32)
    state = background.reshape(tile_cells, channels).astype(jnp.float32) + assimilated
    state = state.astype(jnp.bfloat16).reshape(height, breadth, channels)
    state_rim = widen(state, 2)
    cotangent_rim = widen(cotangent, 1)
    first_pre = conv_three(state_rim, w_first)
    state_near = state_rim[1:-1, 1:-1].astype(jnp.float32)
    hidden = inside_rows((state_near + activate(first_pre)).astype(jnp.bfloat16))
    encoded = conv_stride(hidden, w_second).astype(jnp.bfloat16)
    hidden_grad = conv_stride_back(cotangent_rim, w_second)
    first_pre_again = lax.optimization_barrier(first_pre)
    first_grad = inside_rows(activate_back(first_pre_again, hidden_grad).astype(jnp.bfloat16))
    state_grad = hidden_grad[1:-1, 1:-1] + conv_three_back(first_grad, w_first)
    state_grad = state_grad.astype(jnp.bfloat16).reshape(tile_cells, channels)
    arrived_grad = lax.dot_general(
        cell_match, state_grad, (((0,), (0,)), ((), ())), preferred_element_type=jnp.float32
    )
    slot_back = activate_back(slot_pre, arrived_grad).astype(jnp.bfloat16)
    slot_grad = lax.dot_general(
        slot_back, w_station, (((1,), (1,)), ((), ())), preferred_element_type=jnp.float32
    ).astype(jnp.bfloat16)
    weight_term = lax.dot_general(
        got_obs, slot_back, (((0,), (0,)), ((), ())), preferred_element_type=jnp.float32
    )
    returned = send_back(slot_grad, lon_count, lat_count, capacity)
    station_grad = lax.dot_general(
        slot_pick, returned, (((0,), (0,)), ((), ())), preferred_element_type=jnp.float32
    ).astype(jnp.bfloat16)
    weight_grad = sum_over_devices(weight_term, tile_count)
    weight_grad = weight_grad * (1.0 / math.sqrt(station_count * tile_count))
    return (encoded, station_grad, weight_grad)


def solution(mesh):
    in_specs = (
        P("lat", "lon", None),
        P(("lon", "lat"), None),
        P(),
        P(),
        P(),
        P("lat", "lon", None),
        P(("lon", "lat"), None),
        P(("lon", "lat")),
    )
    out_specs = (P("lat", "lon", None), P(("lon", "lat"), None), P())
    return jax.shard_map(
        on_device, mesh=mesh, in_specs=in_specs, out_specs=out_specs, check_vma=False
    )
```

```python
import math

import jax
import jax.numpy as jnp
from jax import lax
from jax.sharding import PartitionSpec as P

def padded_2(cells, sides, width, closed):
    for axis, dim in sides:
        count = lax.axis_size(axis)
        ends = count if closed else count - 1
        head = lax.slice_in_dim(cells, 0, width, axis=dim)
        tail = lax.slice_in_dim(cells, cells.shape[dim] - width, cells.shape[dim], axis=dim)
        cells = jnp.concatenate(
            [
                lax.ppermute(tail, axis, [(i, (i + 1) % count) for i in range(ends)]),
                cells,
                lax.ppermute(head, axis, [((i + 1) % count, i) for i in range(ends)]),
            ],
            axis=dim,
        )
    return cells


def activate(values):
    return jax.nn.gelu(values, approximate=True)


def activate_back(values, upstream):
    return jax.vjp(activate, values)[1](upstream)[0]


def widen(grid_field, width):
    lon_sides = padded_2(grid_field, (("lon", 1),), width, True)
    return padded_2(lon_sides, (("lat", 0),), width, False)


def inside_rows(field):
    lat_index = lax.axis_index("lat")
    last = lax.axis_size("lat") - 1
    rows = jnp.arange(field.shape[0])[:, None, None]
    outside = ((rows == 0) & (lat_index == 0)) | ((rows == field.shape[0] - 1) & (lat_index == last))
    return jnp.where(outside, jnp.zeros_like(field), field)


def conv_valid(padded, kernel, stride, dilation, spec, rim=0):
    result = lax.conv_general_dilated(
        padded[None],
        kernel,
        (stride, stride),
        ((rim, rim), (rim, rim)),
        lhs_dilation=(dilation, dilation),
        dimension_numbers=("NHWC", spec, "NHWC"),
        preferred_element_type=jnp.float32,
    )
    return result[0]


def conv_three(padded, weight):
    return conv_valid(padded, weight, 1, 1, "HWIO")


def conv_stride(padded, weight):
    return conv_valid(padded, weight, 2, 1, "HWIO")


def conv_three_back(extended, weight):
    return conv_valid(extended, weight[::-1, ::-1], 1, 1, "HWOI")


def conv_stride_back(extended, weight):
    return conv_valid(extended, weight[::-1, ::-1], 1, 2, "HWOI", 1)


def send_out(payload, cell_ids, lon_count, lat_count, capacity):
    feature_width = payload.shape[1]
    tile_count = lon_count * lat_count
    shifted = cell_ids.reshape(tile_count, capacity) + 1
    high = (shifted // 64).astype(payload.dtype)
    low = (shifted % 64).astype(payload.dtype)
    packed = jnp.concatenate(
        [payload.reshape(tile_count, capacity * feature_width), high, low], axis=1
    )
    got = lax.all_to_all(packed, ("lon", "lat"), split_axis=0, concat_axis=0, tiled=True)
    got_load = got[:, : capacity * feature_width].reshape(-1, feature_width)
    got_high = got[:, capacity * feature_width : capacity * (feature_width + 1)]
    got_low = got[:, capacity * (feature_width + 1) :]
    got_cells = got_high.astype(jnp.int32) * 64 + got_low.astype(jnp.int32) - 1
    return (got_load, got_cells.reshape(-1))


def send_back(reply_rows, lon_count, lat_count, capacity):
    feature_width = reply_rows.shape[1]
    returned = lax.all_to_all(
        reply_rows.reshape(lon_count * lat_count, capacity, feature_width),
        ("lon", "lat"),
        split_axis=0,
        concat_axis=0,
        tiled=True,
    )
    return returned.reshape(-1, feature_width)


def sum_over_devices(term, count):
    rows, width = term.shape
    if rows % count != 0:
        return lax.psum(term, ("lon", "lat"))
    pieces = term.reshape(count, rows // count, width)
    gathered = lax.all_to_all(pieces, ("lon", "lat"), split_axis=0, concat_axis=0, tiled=True)
    own = jnp.sum(gathered, axis=0, keepdims=True)
    spread = jnp.broadcast_to(own, (count, rows // count, width))
    whole = lax.all_to_all(spread, ("lon", "lat"), split_axis=0, concat_axis=0, tiled=True)
    return whole.reshape(rows, width)


def send_back_with_sum(reply_rows, term, count, capacity):
    feature_width = reply_rows.shape[1]
    rows, width = term.shape
    if rows % count != 0:
        returned = send_back(reply_rows, count, 1, capacity)
        return returned, sum_over_devices(term, count)
    span = capacity * feature_width
    packed = jnp.concatenate(
        [
            reply_rows.astype(jnp.float32).reshape(count, span),
            term.reshape(count, rows // count * width),
        ],
        axis=1,
    )
    got = lax.all_to_all(packed, ("lon", "lat"), split_axis=0, concat_axis=0, tiled=True)
    returned = got[:, :span].astype(reply_rows.dtype).reshape(-1, feature_width)
    own = jnp.sum(got[:, span:], axis=0).reshape(1, rows // count, width)
    spread = jnp.broadcast_to(own, (count, rows // count, width))
    whole = lax.all_to_all(spread, ("lon", "lat"), split_axis=0, concat_axis=0, tiled=True)
    return returned, whole.reshape(rows, width)


def on_device(
    background, observations, w_station, w_first, w_second, cotangent, station_tile, station_cell
):
    lon_count = lax.axis_size("lon")
    lat_count = lax.axis_size("lat")
    tile_count = lon_count * lat_count
    height, breadth, channels = background.shape
    tile_cells = height * breadth
    station_count = observations.shape[0]
    capacity = 2 * station_count // tile_count
    slot_total = tile_count * capacity
    target_tile = station_tile[:, 0]
    matches = (target_tile[:, None] == jnp.arange(tile_count, dtype=jnp.int32)[None, :]).astype(
        jnp.bfloat16
    )
    order = jnp.arange(station_count, dtype=jnp.int32)
    before = (order[:, None] > order[None, :]).astype(jnp.bfloat16)
    earlier = jnp.dot(before, matches, preferred_element_type=jnp.float32)
    rank = jnp.sum(earlier * matches.astype(jnp.float32), axis=1).astype(jnp.int32)
    flat_slot = target_tile * capacity + rank
    slot_hit = jnp.arange(slot_total, dtype=jnp.int32)[:, None] == flat_slot[None, :]
    slot_pick = slot_hit.astype(jnp.bfloat16)
    send_cells = jnp.sum(jnp.where(slot_hit, station_cell[None, :] + 1, 0), axis=1) - 1
    send_rows = jnp.dot(slot_pick, observations, preferred_element_type=jnp.float32).astype(
        jnp.bfloat16
    )
    got_obs, got_cells = send_out(send_rows, send_cells, lon_count, lat_count, capacity)
    slot_pre = jnp.dot(got_obs, w_station, preferred_element_type=jnp.float32)
    slot_embedded = activate(slot_pre).astype(jnp.bfloat16)
    cell_match = (jnp.arange(tile_cells, dtype=jnp.int32)[:, None] == got_cells[None, :]).astype(
        jnp.bfloat16
    )
    assimilated = jnp.dot(cell_match, slot_embedded, preferred_element_type=jnp.float32)
    state = background.reshape(tile_cells, channels).astype(jnp.float32) + assimilated
    state = state.astype(jnp.bfloat16).reshape(height, breadth, channels)
    state_rim = widen(state, 2)
    cotangent_rim = widen(cotangent, 1)
    first_pre = conv_three(state_rim, w_first)
    state_near = state_rim[1:-1, 1:-1].astype(jnp.float32)
    hidden = inside_rows((state_near + activate(first_pre)).astype(jnp.bfloat16))
    encoded = conv_stride(hidden, w_second).astype(jnp.bfloat16)
    hidden_grad = conv_stride_back(cotangent_rim, w_second)
    first_pre_again = lax.optimization_barrier(first_pre)
    first_grad = inside_rows(activate_back(first_pre_again, hidden_grad).astype(jnp.bfloat16))
    state_grad = hidden_grad[1:-1, 1:-1] + conv_three_back(first_grad, w_first)
    state_grad = state_grad.astype(jnp.bfloat16).reshape(tile_cells, channels)
    arrived_grad = lax.dot_general(
        cell_match, state_grad, (((0,), (0,)), ((), ())), preferred_element_type=jnp.float32
    )
    slot_back = activate_back(slot_pre, arrived_grad).astype(jnp.bfloat16)
    slot_grad = lax.dot_general(
        slot_back, w_station, (((1,), (1,)), ((), ())), preferred_element_type=jnp.float32
    ).astype(jnp.bfloat16)
    weight_term = lax.dot_general(
        got_obs, slot_back, (((0,), (0,)), ((), ())), preferred_element_type=jnp.float32
    )
    returned, weight_grad = send_back_with_sum(slot_grad, weight_term, tile_count, capacity)
    station_grad = lax.dot_general(
        slot_pick, returned, (((0,), (0,)), ((), ())), preferred_element_type=jnp.float32
    ).astype(jnp.bfloat16)
    weight_grad = weight_grad * (1.0 / math.sqrt(station_count * tile_count))
    return (encoded, station_grad, weight_grad)


def solution(mesh):
    in_specs = (
        P("lat", "lon", None),
        P(("lon", "lat"), None),
        P(),
        P(),
        P(),
        P("lat", "lon", None),
        P(("lon", "lat"), None),
        P(("lon", "lat")),
    )
    out_specs = (P("lat", "lon", None), P(("lon", "lat"), None), P())
    return jax.shard_map(
        on_device, mesh=mesh, in_specs=in_specs, out_specs=out_specs, check_vma=False
    )
```

```python
import math

import jax
import jax.numpy as jnp
from jax import lax
from jax.sharding import PartitionSpec as P

def padded_2(cells, sides, width, closed):
    for axis, dim in sides:
        count = lax.axis_size(axis)
        ends = count if closed else count - 1
        head = lax.slice_in_dim(cells, 0, width, axis=dim)
        tail = lax.slice_in_dim(cells, cells.shape[dim] - width, cells.shape[dim], axis=dim)
        cells = jnp.concatenate(
            [
                lax.ppermute(tail, axis, [(i, (i + 1) % count) for i in range(ends)]),
                cells,
                lax.ppermute(head, axis, [((i + 1) % count, i) for i in range(ends)]),
            ],
            axis=dim,
        )
    return cells


def activate(values):
    return jax.nn.gelu(values, approximate=True)


def activate_back(values, upstream):
    return jax.vjp(activate, values)[1](upstream)[0]


def widen(grid_field, width):
    lon_sides = padded_2(grid_field, (("lon", 1),), width, True)
    return padded_2(lon_sides, (("lat", 0),), width, False)


def inside_rows(field):
    lat_index = lax.axis_index("lat")
    last = lax.axis_size("lat") - 1
    rows = jnp.arange(field.shape[0])[:, None, None]
    outside = ((rows == 0) & (lat_index == 0)) | ((rows == field.shape[0] - 1) & (lat_index == last))
    return jnp.where(outside, jnp.zeros_like(field), field)


def conv_valid(padded, kernel, stride, dilation, spec, rim=0):
    result = lax.conv_general_dilated(
        padded[None],
        kernel,
        (stride, stride),
        ((rim, rim), (rim, rim)),
        lhs_dilation=(dilation, dilation),
        dimension_numbers=("NHWC", spec, "NHWC"),
        preferred_element_type=jnp.float32,
    )
    return result[0]


def conv_three(padded, weight):
    return conv_valid(padded, weight, 1, 1, "HWIO")


def conv_stride(padded, weight):
    return conv_valid(padded, weight, 2, 1, "HWIO")


def conv_three_back(extended, weight):
    return conv_valid(extended, weight[::-1, ::-1], 1, 1, "HWOI")


def conv_stride_back(extended, weight):
    return conv_valid(extended, weight[::-1, ::-1], 1, 2, "HWOI", 1)


def send_out(payload, cell_ids, lon_count, lat_count, capacity):
    feature_width = payload.shape[1]
    tile_count = lon_count * lat_count
    shifted = cell_ids.reshape(tile_count, capacity) + 1
    high = (shifted // 64).astype(payload.dtype)
    low = (shifted % 64).astype(payload.dtype)
    packed = jnp.concatenate(
        [payload.reshape(tile_count, capacity * feature_width), high, low], axis=1
    )
    got = lax.all_to_all(packed, ("lon", "lat"), split_axis=0, concat_axis=0, tiled=True)
    got_load = got[:, : capacity * feature_width].reshape(-1, feature_width)
    got_high = got[:, capacity * feature_width : capacity * (feature_width + 1)]
    got_low = got[:, capacity * (feature_width + 1) :]
    got_cells = got_high.astype(jnp.int32) * 64 + got_low.astype(jnp.int32) - 1
    return (got_load, got_cells.reshape(-1))


def send_back(reply_rows, lon_count, lat_count, capacity):
    feature_width = reply_rows.shape[1]
    returned = lax.all_to_all(
        reply_rows.reshape(lon_count * lat_count, capacity, feature_width),
        ("lon", "lat"),
        split_axis=0,
        concat_axis=0,
        tiled=True,
    )
    return returned.reshape(-1, feature_width)


def sum_over_devices(term, count):
    rows, width = term.shape
    if rows % count != 0:
        return lax.psum(term, ("lon", "lat"))
    pieces = term.reshape(count, rows // count, width)
    gathered = lax.all_to_all(pieces, ("lon", "lat"), split_axis=0, concat_axis=0, tiled=True)
    own = jnp.sum(gathered, axis=0, keepdims=True)
    spread = jnp.broadcast_to(own, (count, rows // count, width))
    whole = lax.all_to_all(spread, ("lon", "lat"), split_axis=0, concat_axis=0, tiled=True)
    return whole.reshape(rows, width)


def send_back_with_sum(reply_rows, term, count, capacity):
    feature_width = reply_rows.shape[1]
    rows, width = term.shape
    if rows % count != 0:
        returned = send_back(reply_rows, count, 1, capacity)
        return returned, sum_over_devices(term, count)
    span = capacity * feature_width
    piece = rows // count * width
    term_pieces = term.reshape(count, piece)
    term_high = term_pieces.astype(reply_rows.dtype)
    term_low = (term_pieces - term_high.astype(jnp.float32)).astype(reply_rows.dtype)
    packed = jnp.concatenate(
        [reply_rows.reshape(count, span), term_high, term_low], axis=1
    )
    got = lax.all_to_all(packed, ("lon", "lat"), split_axis=0, concat_axis=0, tiled=True)
    returned = got[:, :span].reshape(-1, feature_width)
    got_high = got[:, span : span + piece].astype(jnp.float32)
    got_low = got[:, span + piece :].astype(jnp.float32)
    own = jnp.sum(got_high + got_low, axis=0).reshape(1, rows // count, width)
    spread = jnp.broadcast_to(own, (count, rows // count, width))
    whole = lax.all_to_all(spread, ("lon", "lat"), split_axis=0, concat_axis=0, tiled=True)
    return returned, whole.reshape(rows, width)


def on_device(
    background, observations, w_station, w_first, w_second, cotangent, station_tile, station_cell
):
    lon_count = lax.axis_size("lon")
    lat_count = lax.axis_size("lat")
    tile_count = lon_count * lat_count
    height, breadth, channels = background.shape
    tile_cells = height * breadth
    station_count = observations.shape[0]
    capacity = 2 * station_count // tile_count
    slot_total = tile_count * capacity
    target_tile = station_tile[:, 0]
    matches = (target_tile[:, None] == jnp.arange(tile_count, dtype=jnp.int32)[None, :]).astype(
        jnp.bfloat16
    )
    order = jnp.arange(station_count, dtype=jnp.int32)
    before = (order[:, None] > order[None, :]).astype(jnp.bfloat16)
    earlier = jnp.dot(before, matches, preferred_element_type=jnp.float32)
    rank = jnp.sum(earlier * matches.astype(jnp.float32), axis=1).astype(jnp.int32)
    flat_slot = target_tile * capacity + rank
    slot_hit = jnp.arange(slot_total, dtype=jnp.int32)[:, None] == flat_slot[None, :]
    slot_pick = slot_hit.astype(jnp.bfloat16)
    send_cells = jnp.sum(jnp.where(slot_hit, station_cell[None, :] + 1, 0), axis=1) - 1
    send_rows = jnp.dot(slot_pick, observations, preferred_element_type=jnp.float32).astype(
        jnp.bfloat16
    )
    got_obs, got_cells = send_out(send_rows, send_cells, lon_count, lat_count, capacity)
    slot_pre = jnp.dot(got_obs, w_station, preferred_element_type=jnp.float32)
    slot_embedded = activate(slot_pre).astype(jnp.bfloat16)
    cell_match = (jnp.arange(tile_cells, dtype=jnp.int32)[:, None] == got_cells[None, :]).astype(
        jnp.bfloat16
    )
    assimilated = jnp.dot(cell_match, slot_embedded, preferred_element_type=jnp.float32)
    state = background.reshape(tile_cells, channels).astype(jnp.float32) + assimilated
    state = state.astype(jnp.bfloat16).reshape(height, breadth, channels)
    state_rim = widen(state, 2)
    cotangent_rim = widen(cotangent, 1)
    first_pre = conv_three(state_rim, w_first)
    state_near = state_rim[1:-1, 1:-1].astype(jnp.float32)
    hidden = inside_rows((state_near + activate(first_pre)).astype(jnp.bfloat16))
    encoded = conv_stride(hidden, w_second).astype(jnp.bfloat16)
    hidden_grad = conv_stride_back(cotangent_rim, w_second)
    first_pre_again = lax.optimization_barrier(first_pre)
    first_grad = inside_rows(activate_back(first_pre_again, hidden_grad).astype(jnp.bfloat16))
    state_grad = hidden_grad[1:-1, 1:-1] + conv_three_back(first_grad, w_first)
    state_grad = state_grad.astype(jnp.bfloat16).reshape(tile_cells, channels)
    arrived_grad = lax.dot_general(
        cell_match, state_grad, (((0,), (0,)), ((), ())), preferred_element_type=jnp.float32
    )
    slot_back = activate_back(slot_pre, arrived_grad).astype(jnp.bfloat16)
    slot_grad = lax.dot_general(
        slot_back, w_station, (((1,), (1,)), ((), ())), preferred_element_type=jnp.float32
    ).astype(jnp.bfloat16)
    weight_term = lax.dot_general(
        got_obs, slot_back, (((0,), (0,)), ((), ())), preferred_element_type=jnp.float32
    )
    returned, weight_grad = send_back_with_sum(slot_grad, weight_term, tile_count, capacity)
    station_grad = lax.dot_general(
        slot_pick, returned, (((0,), (0,)), ((), ())), preferred_element_type=jnp.float32
    ).astype(jnp.bfloat16)
    weight_grad = weight_grad * (1.0 / math.sqrt(station_count * tile_count))
    return (encoded, station_grad, weight_grad)


def solution(mesh):
    in_specs = (
        P("lat", "lon", None),
        P(("lon", "lat"), None),
        P(),
        P(),
        P(),
        P("lat", "lon", None),
        P(("lon", "lat"), None),
        P(("lon", "lat")),
    )
    out_specs = (P("lat", "lon", None), P(("lon", "lat"), None), P())
    return jax.shard_map(
        on_device, mesh=mesh, in_specs=in_specs, out_specs=out_specs, check_vma=False
    )
```

```python
import math

import jax
import jax.numpy as jnp
from jax import lax
from jax.sharding import PartitionSpec as P

def activate(values):
    return jax.nn.gelu(values, approximate=True)


def activate_back(values, upstream):
    return jax.vjp(activate, values)[1](upstream)[0]


def exchange(fields, axis, dim, closed):
    count = lax.axis_size(axis)
    ends = count if closed else count - 1
    heads = [lax.slice_in_dim(f, 0, w, axis=dim) for f, w in fields]
    tails = [lax.slice_in_dim(f, f.shape[dim] - w, f.shape[dim], axis=dim) for f, w in fields]

    def pack(parts):
        return jnp.concatenate([p.reshape(-1, p.shape[-1]) for p in parts], axis=0)

    def unpack(packed, like):
        pieces, at = [], 0
        for p in like:
            rows = p.size // p.shape[-1]
            pieces.append(packed[at : at + rows].reshape(p.shape))
            at += rows
        return pieces

    got_tails = unpack(
        lax.ppermute(pack(tails), axis, [(i, (i + 1) % count) for i in range(ends)]), tails
    )
    got_heads = unpack(
        lax.ppermute(pack(heads), axis, [((i + 1) % count, i) for i in range(ends)]), heads
    )
    return [
        jnp.concatenate([t, f, h], axis=dim)
        for (f, _), t, h in zip(fields, got_tails, got_heads)
    ]


def widen_both(state, cotangent):
    state_lon, cotangent_lon = exchange([(state, 2), (cotangent, 1)], "lon", 1, True)
    return exchange([(state_lon, 2), (cotangent_lon, 1)], "lat", 0, False)


def inside_rows(field):
    lat_index = lax.axis_index("lat")
    last = lax.axis_size("lat") - 1
    rows = jnp.arange(field.shape[0])[:, None, None]
    outside = ((rows == 0) & (lat_index == 0)) | ((rows == field.shape[0] - 1) & (lat_index == last))
    return jnp.where(outside, jnp.zeros_like(field), field)


def conv_valid(padded, kernel, stride, dilation, spec, rim=0):
    result = lax.conv_general_dilated(
        padded[None],
        kernel,
        (stride, stride),
        ((rim, rim), (rim, rim)),
        lhs_dilation=(dilation, dilation),
        dimension_numbers=("NHWC", spec, "NHWC"),
        preferred_element_type=jnp.float32,
    )
    return result[0]


def conv_three(padded, weight):
    return conv_valid(padded, weight, 1, 1, "HWIO")


def conv_stride(padded, weight):
    return conv_valid(padded, weight, 2, 1, "HWIO")


def conv_three_back(extended, weight):
    return conv_valid(extended, weight[::-1, ::-1], 1, 1, "HWOI")


def conv_stride_back(extended, weight):
    return conv_valid(extended, weight[::-1, ::-1], 1, 2, "HWOI", 1)


def send_out(payload, cell_ids, lon_count, lat_count, capacity):
    feature_width = payload.shape[1]
    tile_count = lon_count * lat_count
    shifted = cell_ids.reshape(tile_count, capacity) + 1
    high = (shifted // 64).astype(payload.dtype)
    low = (shifted % 64).astype(payload.dtype)
    packed = jnp.concatenate(
        [payload.reshape(tile_count, capacity * feature_width), high, low], axis=1
    )
    got = lax.all_to_all(packed, ("lon", "lat"), split_axis=0, concat_axis=0, tiled=True)
    got_load = got[:, : capacity * feature_width].reshape(-1, feature_width)
    got_high = got[:, capacity * feature_width : capacity * (feature_width + 1)]
    got_low = got[:, capacity * (feature_width + 1) :]
    got_cells = got_high.astype(jnp.int32) * 64 + got_low.astype(jnp.int32) - 1
    return (got_load, got_cells.reshape(-1))


def send_back(reply_rows, lon_count, lat_count, capacity):
    feature_width = reply_rows.shape[1]
    returned = lax.all_to_all(
        reply_rows.reshape(lon_count * lat_count, capacity, feature_width),
        ("lon", "lat"),
        split_axis=0,
        concat_axis=0,
        tiled=True,
    )
    return returned.reshape(-1, feature_width)


def sum_over_devices(term, count):
    rows, width = term.shape
    if rows % count != 0:
        return lax.psum(term, ("lon", "lat"))
    pieces = term.reshape(count, rows // count, width)
    gathered = lax.all_to_all(pieces, ("lon", "lat"), split_axis=0, concat_axis=0, tiled=True)
    own = jnp.sum(gathered, axis=0, keepdims=True)
    spread = jnp.broadcast_to(own, (count, rows // count, width))
    whole = lax.all_to_all(spread, ("lon", "lat"), split_axis=0, concat_axis=0, tiled=True)
    return whole.reshape(rows, width)


def on_device(
    background, observations, w_station, w_first, w_second, cotangent, station_tile, station_cell
):
    lon_count = lax.axis_size("lon")
    lat_count = lax.axis_size("lat")
    tile_count = lon_count * lat_count
    height, breadth, channels = background.shape
    tile_cells = height * breadth
    station_count = observations.shape[0]
    capacity = 2 * station_count // tile_count
    slot_total = tile_count * capacity
    target_tile = station_tile[:, 0]
    matches = (target_tile[:, None] == jnp.arange(tile_count, dtype=jnp.int32)[None, :]).astype(
        jnp.bfloat16
    )
    order = jnp.arange(station_count, dtype=jnp.int32)
    before = (order[:, None] > order[None, :]).astype(jnp.bfloat16)
    earlier = jnp.dot(before, matches, preferred_element_type=jnp.float32)
    rank = jnp.sum(earlier * matches.astype(jnp.float32), axis=1).astype(jnp.int32)
    flat_slot = target_tile * capacity + rank
    slot_hit = jnp.arange(slot_total, dtype=jnp.int32)[:, None] == flat_slot[None, :]
    slot_pick = slot_hit.astype(jnp.bfloat16)
    send_cells = jnp.sum(jnp.where(slot_hit, station_cell[None, :] + 1, 0), axis=1) - 1
    send_rows = jnp.dot(slot_pick, observations, preferred_element_type=jnp.float32).astype(
        jnp.bfloat16
    )
    got_obs, got_cells = send_out(send_rows, send_cells, lon_count, lat_count, capacity)
    slot_pre = jnp.dot(got_obs, w_station, preferred_element_type=jnp.float32)
    slot_embedded = activate(slot_pre).astype(jnp.bfloat16)
    cell_match = (jnp.arange(tile_cells, dtype=jnp.int32)[:, None] == got_cells[None, :]).astype(
        jnp.bfloat16
    )
    assimilated = jnp.dot(cell_match, slot_embedded, preferred_element_type=jnp.float32)
    state = background.reshape(tile_cells, channels).astype(jnp.float32) + assimilated
    state = state.astype(jnp.bfloat16).reshape(height, breadth, channels)
    state_rim, cotangent_rim = widen_both(state, cotangent)
    first_pre = conv_three(state_rim, w_first)
    state_near = state_rim[1:-1, 1:-1].astype(jnp.float32)
    hidden = inside_rows((state_near + activate(first_pre)).astype(jnp.bfloat16))
    encoded = conv_stride(hidden, w_second).astype(jnp.bfloat16)
    hidden_grad = conv_stride_back(cotangent_rim, w_second)
    first_pre_again = lax.optimization_barrier(first_pre)
    first_grad = inside_rows(activate_back(first_pre_again, hidden_grad).astype(jnp.bfloat16))
    state_grad = hidden_grad[1:-1, 1:-1] + conv_three_back(first_grad, w_first)
    state_grad = state_grad.astype(jnp.bfloat16).reshape(tile_cells, channels)
    arrived_grad = lax.dot_general(
        cell_match, state_grad, (((0,), (0,)), ((), ())), preferred_element_type=jnp.float32
    )
    slot_back = activate_back(slot_pre, arrived_grad).astype(jnp.bfloat16)
    slot_grad = lax.dot_general(
        slot_back, w_station, (((1,), (1,)), ((), ())), preferred_element_type=jnp.float32
    ).astype(jnp.bfloat16)
    weight_term = lax.dot_general(
        got_obs, slot_back, (((0,), (0,)), ((), ())), preferred_element_type=jnp.float32
    )
    returned = send_back(slot_grad, lon_count, lat_count, capacity)
    returned, weight_term = lax.optimization_barrier((returned, weight_term))
    station_grad = lax.dot_general(
        slot_pick, returned, (((0,), (0,)), ((), ())), preferred_element_type=jnp.float32
    ).astype(jnp.bfloat16)
    weight_grad = sum_over_devices(weight_term, tile_count)
    weight_grad = weight_grad * (1.0 / math.sqrt(station_count * tile_count))
    return (encoded, station_grad, weight_grad)


def solution(mesh):
    in_specs = (
        P("lat", "lon", None),
        P(("lon", "lat"), None),
        P(),
        P(),
        P(),
        P("lat", "lon", None),
        P(("lon", "lat"), None),
        P(("lon", "lat")),
    )
    out_specs = (P("lat", "lon", None), P(("lon", "lat"), None), P())
    return jax.shard_map(
        on_device, mesh=mesh, in_specs=in_specs, out_specs=out_specs, check_vma=False
    )
```

```python
import math

import jax
import jax.numpy as jnp
from jax import lax
from jax.sharding import PartitionSpec as P

def padded_2(cells, sides, width, closed):
    for axis, dim in sides:
        count = lax.axis_size(axis)
        ends = count if closed else count - 1
        head = lax.slice_in_dim(cells, 0, width, axis=dim)
        tail = lax.slice_in_dim(cells, cells.shape[dim] - width, cells.shape[dim], axis=dim)
        cells = jnp.concatenate(
            [
                lax.ppermute(tail, axis, [(i, (i + 1) % count) for i in range(ends)]),
                cells,
                lax.ppermute(head, axis, [((i + 1) % count, i) for i in range(ends)]),
            ],
            axis=dim,
        )
    return cells


def activate(values):
    return jax.nn.gelu(values, approximate=True)


def activate_back(values, upstream):
    return jax.vjp(activate, values)[1](upstream)[0]


def widen(grid_field, width):
    lon_sides = padded_2(grid_field, (("lon", 1),), width, True)
    return padded_2(lon_sides, (("lat", 0),), width, False)


def inside_rows(field):
    lat_index = lax.axis_index("lat")
    last = lax.axis_size("lat") - 1
    rows = jnp.arange(field.shape[0])[:, None, None]
    outside = ((rows == 0) & (lat_index == 0)) | ((rows == field.shape[0] - 1) & (lat_index == last))
    return jnp.where(outside, jnp.zeros_like(field), field)


def conv_valid(padded, kernel, stride, dilation, spec, rim=0):
    result = lax.conv_general_dilated(
        padded[None],
        kernel,
        (stride, stride),
        ((rim, rim), (rim, rim)),
        lhs_dilation=(dilation, dilation),
        dimension_numbers=("NHWC", spec, "NHWC"),
        preferred_element_type=jnp.float32,
    )
    return result[0]


def conv_three(padded, weight):
    return conv_valid(padded, weight, 1, 1, "HWIO")


def conv_stride(padded, weight):
    return conv_valid(padded, weight, 2, 1, "HWIO")


def conv_three_back(extended, weight):
    return conv_valid(extended, weight[::-1, ::-1], 1, 1, "HWOI")


def conv_stride_back(extended, weight):
    return conv_valid(extended, weight[::-1, ::-1], 1, 2, "HWOI", 1)


def send_out(payload, cell_ids, lon_count, lat_count, capacity):
    feature_width = payload.shape[1]
    tile_count = lon_count * lat_count
    shifted = cell_ids.reshape(tile_count, capacity) + 1
    high = (shifted // 64).astype(payload.dtype)
    low = (shifted % 64).astype(payload.dtype)
    packed = jnp.concatenate(
        [payload.reshape(tile_count, capacity * feature_width), high, low], axis=1
    )
    got = lax.all_to_all(packed, ("lon", "lat"), split_axis=0, concat_axis=0, tiled=True)
    got_load = got[:, : capacity * feature_width].reshape(-1, feature_width)
    got_high = got[:, capacity * feature_width : capacity * (feature_width + 1)]
    got_low = got[:, capacity * (feature_width + 1) :]
    got_cells = got_high.astype(jnp.int32) * 64 + got_low.astype(jnp.int32) - 1
    return (got_load, got_cells.reshape(-1))


def send_back(reply_rows, lon_count, lat_count, capacity):
    feature_width = reply_rows.shape[1]
    returned = lax.all_to_all(
        reply_rows.reshape(lon_count * lat_count, capacity, feature_width),
        ("lon", "lat"),
        split_axis=0,
        concat_axis=0,
        tiled=True,
    )
    return returned.reshape(-1, feature_width)


def sum_over_devices(term, count):
    rows, width = term.shape
    if rows % count != 0:
        return lax.psum(term, ("lon", "lat"))
    pieces = term.reshape(count, rows // count, width)
    gathered = lax.all_to_all(pieces, ("lon", "lat"), split_axis=0, concat_axis=0, tiled=True)
    own = jnp.sum(gathered, axis=0, keepdims=True)
    spread = jnp.broadcast_to(own, (count, rows // count, width))
    whole = lax.all_to_all(spread, ("lon", "lat"), split_axis=0, concat_axis=0, tiled=True)
    return whole.reshape(rows, width)


def on_device(
    background, observations, w_station, w_first, w_second, cotangent, station_tile, station_cell
):
    lon_count = lax.axis_size("lon")
    lat_count = lax.axis_size("lat")
    tile_count = lon_count * lat_count
    height, breadth, channels = background.shape
    tile_cells = height * breadth
    station_count = observations.shape[0]
    capacity = 2 * station_count // tile_count
    slot_total = tile_count * capacity
    target_tile = station_tile[:, 0]
    matches = (target_tile[:, None] == jnp.arange(tile_count, dtype=jnp.int32)[None, :]).astype(
        jnp.bfloat16
    )
    order = jnp.arange(station_count, dtype=jnp.int32)
    before = (order[:, None] > order[None, :]).astype(jnp.bfloat16)
    earlier = jnp.dot(before, matches, preferred_element_type=jnp.float32)
    rank = jnp.sum(earlier * matches.astype(jnp.float32), axis=1).astype(jnp.int32)
    flat_slot = target_tile * capacity + rank
    slot_hit = jnp.arange(slot_total, dtype=jnp.int32)[:, None] == flat_slot[None, :]
    slot_pick = slot_hit.astype(jnp.bfloat16)
    send_cells = jnp.sum(jnp.where(slot_hit, station_cell[None, :] + 1, 0), axis=1) - 1
    send_rows = jnp.dot(slot_pick, observations, preferred_element_type=jnp.float32).astype(
        jnp.bfloat16
    )
    got_obs, got_cells = send_out(send_rows, send_cells, lon_count, lat_count, capacity)
    cotangent_rim = widen(cotangent, 1)
    hidden_grad = conv_stride_back(cotangent_rim, w_second)
    hidden_grad, got_obs, got_cells = lax.optimization_barrier((hidden_grad, got_obs, got_cells))
    slot_pre = jnp.dot(got_obs, w_station, preferred_element_type=jnp.float32)
    slot_embedded = activate(slot_pre).astype(jnp.bfloat16)
    cell_match = (jnp.arange(tile_cells, dtype=jnp.int32)[:, None] == got_cells[None, :]).astype(
        jnp.bfloat16
    )
    assimilated = jnp.dot(cell_match, slot_embedded, preferred_element_type=jnp.float32)
    state = background.reshape(tile_cells, channels).astype(jnp.float32) + assimilated
    state = state.astype(jnp.bfloat16).reshape(height, breadth, channels)
    state_rim = widen(state, 2)
    first_pre = conv_three(state_rim, w_first)
    state_near = state_rim[1:-1, 1:-1].astype(jnp.float32)
    hidden = inside_rows((state_near + activate(first_pre)).astype(jnp.bfloat16))
    encoded = conv_stride(hidden, w_second).astype(jnp.bfloat16)
    first_pre_again = lax.optimization_barrier(first_pre)
    first_grad = inside_rows(activate_back(first_pre_again, hidden_grad).astype(jnp.bfloat16))
    state_grad = hidden_grad[1:-1, 1:-1] + conv_three_back(first_grad, w_first)
    state_grad = state_grad.astype(jnp.bfloat16).reshape(tile_cells, channels)
    arrived_grad = lax.dot_general(
        cell_match, state_grad, (((0,), (0,)), ((), ())), preferred_element_type=jnp.float32
    )
    slot_back = activate_back(slot_pre, arrived_grad).astype(jnp.bfloat16)
    slot_grad = lax.dot_general(
        slot_back, w_station, (((1,), (1,)), ((), ())), preferred_element_type=jnp.float32
    ).astype(jnp.bfloat16)
    weight_term = lax.dot_general(
        got_obs, slot_back, (((0,), (0,)), ((), ())), preferred_element_type=jnp.float32
    )
    returned = send_back(slot_grad, lon_count, lat_count, capacity)
    station_grad = lax.dot_general(
        slot_pick, returned, (((0,), (0,)), ((), ())), preferred_element_type=jnp.float32
    ).astype(jnp.bfloat16)
    weight_grad = sum_over_devices(weight_term, tile_count)
    weight_grad = weight_grad * (1.0 / math.sqrt(station_count * tile_count))
    return (encoded, station_grad, weight_grad)


def solution(mesh):
    in_specs = (
        P("lat", "lon", None),
        P(("lon", "lat"), None),
        P(),
        P(),
        P(),
        P("lat", "lon", None),
        P(("lon", "lat"), None),
        P(("lon", "lat")),
    )
    out_specs = (P("lat", "lon", None), P(("lon", "lat"), None), P())
    return jax.shard_map(
        on_device, mesh=mesh, in_specs=in_specs, out_specs=out_specs, check_vma=False
    )
```

```python
import math

import jax
import jax.numpy as jnp
from jax import lax
from jax.sharding import PartitionSpec as P

def padded_2(cells, sides, width, closed):
    for axis, dim in sides:
        count = lax.axis_size(axis)
        ends = count if closed else count - 1
        head = lax.slice_in_dim(cells, 0, width, axis=dim)
        tail = lax.slice_in_dim(cells, cells.shape[dim] - width, cells.shape[dim], axis=dim)
        cells = jnp.concatenate(
            [
                lax.ppermute(tail, axis, [(i, (i + 1) % count) for i in range(ends)]),
                cells,
                lax.ppermute(head, axis, [((i + 1) % count, i) for i in range(ends)]),
            ],
            axis=dim,
        )
    return cells


def activate(values):
    return jax.nn.gelu(values, approximate=True)


def activate_back(values, upstream):
    return jax.vjp(activate, values)[1](upstream)[0]


def widen(grid_field, width):
    lon_sides = padded_2(grid_field, (("lon", 1),), width, True)
    return padded_2(lon_sides, (("lat", 0),), width, False)


def inside_rows(field):
    lat_index = lax.axis_index("lat")
    last = lax.axis_size("lat") - 1
    rows = jnp.arange(field.shape[0])[:, None, None]
    outside = ((rows == 0) & (lat_index == 0)) | ((rows == field.shape[0] - 1) & (lat_index == last))
    return jnp.where(outside, jnp.zeros_like(field), field)


def conv_valid(padded, kernel, stride, dilation, spec, rim=0):
    result = lax.conv_general_dilated(
        padded[None],
        kernel,
        (stride, stride),
        ((rim, rim), (rim, rim)),
        lhs_dilation=(dilation, dilation),
        dimension_numbers=("NHWC", spec, "NHWC"),
        preferred_element_type=jnp.float32,
    )
    return result[0]


def conv_three(padded, weight):
    return conv_valid(padded, weight, 1, 1, "HWIO")


def conv_stride(padded, weight):
    return conv_valid(padded, weight, 2, 1, "HWIO")


def conv_three_back(extended, weight):
    return conv_valid(extended, weight[::-1, ::-1], 1, 1, "HWOI")


def conv_stride_back(extended, weight):
    return conv_valid(extended, weight[::-1, ::-1], 1, 2, "HWOI", 1)


def send_out(payload, cell_ids, lon_count, lat_count, capacity):
    feature_width = payload.shape[1]
    got_load, got_cells = (
        lax.all_to_all(
            payload.reshape(lon_count * lat_count, capacity, feature_width),
            ("lon", "lat"),
            split_axis=0,
            concat_axis=0,
            tiled=True,
        ),
        lax.all_to_all(
            cell_ids.reshape(lon_count * lat_count, capacity),
            ("lon", "lat"),
            split_axis=0,
            concat_axis=0,
            tiled=True,
        ),
    )
    return (got_load.reshape(-1, feature_width), got_cells.reshape(-1))


def send_back(reply_rows, lon_count, lat_count, capacity):
    feature_width = reply_rows.shape[1]
    returned = lax.all_to_all(
        reply_rows.reshape(lon_count * lat_count, capacity, feature_width),
        ("lon", "lat"),
        split_axis=0,
        concat_axis=0,
        tiled=True,
    )
    return returned.reshape(-1, feature_width)


def sum_over_devices(term, count):
    rows, width = term.shape
    if rows % count != 0:
        return lax.psum(term, ("lon", "lat"))
    pieces = term.reshape(count, rows // count, width)
    gathered = lax.all_to_all(pieces, ("lon", "lat"), split_axis=0, concat_axis=0, tiled=True)
    own = jnp.sum(gathered, axis=0, keepdims=True)
    spread = jnp.broadcast_to(own, (count, rows // count, width))
    whole = lax.all_to_all(spread, ("lon", "lat"), split_axis=0, concat_axis=0, tiled=True)
    return whole.reshape(rows, width)


def on_device(
    background, observations, w_station, w_first, w_second, cotangent, station_tile, station_cell
):
    lon_count = lax.axis_size("lon")
    lat_count = lax.axis_size("lat")
    tile_count = lon_count * lat_count
    height, breadth, channels = background.shape
    tile_cells = height * breadth
    station_count = observations.shape[0]
    capacity = 2 * station_count // tile_count
    slot_total = tile_count * capacity
    target_tile = station_tile[:, 0]
    matches = (target_tile[:, None] == jnp.arange(tile_count, dtype=jnp.int32)[None, :]).astype(
        jnp.bfloat16
    )
    order = jnp.arange(station_count, dtype=jnp.int32)
    before = (order[:, None] > order[None, :]).astype(jnp.bfloat16)
    earlier = jnp.dot(before, matches, preferred_element_type=jnp.float32)
    rank = jnp.sum(earlier * matches.astype(jnp.float32), axis=1).astype(jnp.int32)
    flat_slot = target_tile * capacity + rank
    slot_hit = jnp.arange(slot_total, dtype=jnp.int32)[:, None] == flat_slot[None, :]
    slot_pick = slot_hit.astype(jnp.bfloat16)
    send_cells = jnp.sum(jnp.where(slot_hit, station_cell[None, :] + 1, 0), axis=1) - 1
    send_rows = jnp.dot(slot_pick, observations, preferred_element_type=jnp.float32).astype(
        jnp.bfloat16
    )
    got_obs, got_cells = send_out(send_rows, send_cells, lon_count, lat_count, capacity)
    slot_pre = jnp.dot(got_obs, w_station, preferred_element_type=jnp.float32)
    slot_embedded = activate(slot_pre).astype(jnp.bfloat16)
    cell_match = (jnp.arange(tile_cells, dtype=jnp.int32)[:, None] == got_cells[None, :]).astype(
        jnp.bfloat16
    )
    assimilated = jnp.dot(cell_match, slot_embedded, preferred_element_type=jnp.float32)
    state = background.reshape(tile_cells, channels).astype(jnp.float32) + assimilated
    state = state.astype(jnp.bfloat16).reshape(height, breadth, channels)
    state_rim = widen(state, 2)
    cotangent_rim = widen(cotangent, 1)
    first_pre = conv_three(state_rim, w_first)
    state_near = state_rim[1:-1, 1:-1].astype(jnp.float32)
    hidden = inside_rows((state_near + activate(first_pre)).astype(jnp.bfloat16))
    encoded = conv_stride(hidden, w_second).astype(jnp.bfloat16)
    hidden_grad = conv_stride_back(cotangent_rim, w_second)
    first_pre_again = lax.optimization_barrier(first_pre)
    first_grad = inside_rows(activate_back(first_pre_again, hidden_grad).astype(jnp.bfloat16))
    state_grad = hidden_grad[1:-1, 1:-1] + conv_three_back(first_grad, w_first)
    state_grad = state_grad.astype(jnp.bfloat16).reshape(tile_cells, channels)
    arrived_grad = lax.dot_general(
        cell_match, state_grad, (((0,), (0,)), ((), ())), preferred_element_type=jnp.float32
    )
    slot_back = activate_back(slot_pre, arrived_grad).astype(jnp.bfloat16)
    slot_grad = lax.dot_general(
        slot_back, w_station, (((1,), (1,)), ((), ())), preferred_element_type=jnp.float32
    ).astype(jnp.bfloat16)
    weight_term = lax.dot_general(
        got_obs, slot_back, (((0,), (0,)), ((), ())), preferred_element_type=jnp.float32
    )
    returned = send_back(slot_grad, lon_count, lat_count, capacity)
    returned, weight_term = lax.optimization_barrier((returned, weight_term))
    station_grad = lax.dot_general(
        slot_pick, returned, (((0,), (0,)), ((), ())), preferred_element_type=jnp.float32
    ).astype(jnp.bfloat16)
    weight_grad = sum_over_devices(weight_term, tile_count)
    weight_grad = weight_grad * (1.0 / math.sqrt(station_count * tile_count))
    return (encoded, station_grad, weight_grad)


def solution(mesh):
    in_specs = (
        P("lat", "lon", None),
        P(("lon", "lat"), None),
        P(),
        P(),
        P(),
        P("lat", "lon", None),
        P(("lon", "lat"), None),
        P(("lon", "lat")),
    )
    out_specs = (P("lat", "lon", None), P(("lon", "lat"), None), P())
    return jax.shard_map(
        on_device, mesh=mesh, in_specs=in_specs, out_specs=out_specs, check_vma=False
    )
```

```python
import math

import jax
import jax.numpy as jnp
from jax import lax
from jax.sharding import PartitionSpec as P

def padded_2(cells, sides, width, closed):
    for axis, dim in sides:
        count = lax.axis_size(axis)
        ends = count if closed else count - 1
        head = lax.slice_in_dim(cells, 0, width, axis=dim)
        tail = lax.slice_in_dim(cells, cells.shape[dim] - width, cells.shape[dim], axis=dim)
        cells = jnp.concatenate(
            [
                lax.ppermute(tail, axis, [(i, (i + 1) % count) for i in range(ends)]),
                cells,
                lax.ppermute(head, axis, [((i + 1) % count, i) for i in range(ends)]),
            ],
            axis=dim,
        )
    return cells


def activate(values):
    return jax.nn.gelu(values, approximate=True)


def activate_back(values, upstream):
    return jax.vjp(activate, values)[1](upstream)[0]


def widen(grid_field, width):
    lon_sides = padded_2(grid_field, (("lon", 1),), width, True)
    return padded_2(lon_sides, (("lat", 0),), width, False)


def inside_rows(field):
    lat_index = lax.axis_index("lat")
    last = lax.axis_size("lat") - 1
    rows = jnp.arange(field.shape[0])[:, None, None]
    outside = ((rows == 0) & (lat_index == 0)) | ((rows == field.shape[0] - 1) & (lat_index == last))
    return jnp.where(outside, jnp.zeros_like(field), field)


def conv_valid(padded, kernel, stride, dilation, spec, rim=0):
    result = lax.conv_general_dilated(
        padded[None],
        kernel,
        (stride, stride),
        ((rim, rim), (rim, rim)),
        lhs_dilation=(dilation, dilation),
        dimension_numbers=("NHWC", spec, "NHWC"),
        preferred_element_type=jnp.float32,
    )
    return result[0]


def conv_three(padded, weight):
    return conv_valid(padded, weight, 1, 1, "HWIO")


def conv_stride(padded, weight):
    return conv_valid(padded, weight, 2, 1, "HWIO")


def conv_three_back(extended, weight):
    return conv_valid(extended, weight[::-1, ::-1], 1, 1, "HWOI")


def conv_stride_back(extended, weight):
    return conv_valid(extended, weight[::-1, ::-1], 1, 2, "HWOI", 1)


def send_out(payload, cell_ids, lon_count, lat_count, capacity):
    feature_width = payload.shape[1]
    got_load, got_cells = (
        lax.all_to_all(
            payload.reshape(lon_count * lat_count, capacity, feature_width),
            ("lon", "lat"),
            split_axis=0,
            concat_axis=0,
            tiled=True,
        ),
        lax.all_to_all(
            cell_ids.reshape(lon_count * lat_count, capacity),
            ("lon", "lat"),
            split_axis=0,
            concat_axis=0,
            tiled=True,
        ),
    )
    return (got_load.reshape(-1, feature_width), got_cells.reshape(-1))


def send_back(reply_rows, lon_count, lat_count, capacity):
    feature_width = reply_rows.shape[1]
    returned = lax.all_to_all(
        reply_rows.reshape(lon_count * lat_count, capacity, feature_width),
        ("lon", "lat"),
        split_axis=0,
        concat_axis=0,
        tiled=True,
    )
    return returned.reshape(-1, feature_width)


def sum_over_devices(term, count):
    rows, width = term.shape
    if rows % count != 0:
        return lax.psum(term, ("lon", "lat"))
    pieces = term.reshape(count, rows // count, width)
    gathered = lax.all_to_all(pieces, ("lon", "lat"), split_axis=0, concat_axis=0, tiled=True)
    own = jnp.sum(gathered, axis=0, keepdims=True)
    spread = jnp.broadcast_to(own, (count, rows // count, width))
    whole = lax.all_to_all(spread, ("lon", "lat"), split_axis=0, concat_axis=0, tiled=True)
    return whole.reshape(rows, width)


def on_device(
    background, observations, w_station, w_first, w_second, cotangent, station_tile, station_cell
):
    lon_count = lax.axis_size("lon")
    lat_count = lax.axis_size("lat")
    tile_count = lon_count * lat_count
    height, breadth, channels = background.shape
    tile_cells = height * breadth
    station_count = observations.shape[0]
    capacity = 2 * station_count // tile_count
    slot_total = tile_count * capacity
    target_tile = station_tile[:, 0]
    matches = (target_tile[:, None] == jnp.arange(tile_count, dtype=jnp.int32)[None, :]).astype(
        jnp.bfloat16
    )
    order = jnp.arange(station_count, dtype=jnp.int32)
    before = (order[:, None] > order[None, :]).astype(jnp.bfloat16)
    earlier = jnp.dot(before, matches, preferred_element_type=jnp.float32)
    rank = jnp.sum(earlier * matches.astype(jnp.float32), axis=1).astype(jnp.int32)
    flat_slot = target_tile * capacity + rank
    slot_hit = jnp.arange(slot_total, dtype=jnp.int32)[:, None] == flat_slot[None, :]
    slot_pick = slot_hit.astype(jnp.bfloat16)
    send_cells = jnp.sum(jnp.where(slot_hit, station_cell[None, :] + 1, 0), axis=1) - 1
    send_rows = jnp.dot(slot_pick, observations, preferred_element_type=jnp.float32).astype(
        jnp.bfloat16
    )
    got_obs, got_cells = send_out(send_rows, send_cells, lon_count, lat_count, capacity)
    slot_pre = jnp.dot(got_obs, w_station, preferred_element_type=jnp.float32)
    slot_embedded = activate(slot_pre).astype(jnp.bfloat16)
    cell_match = (jnp.arange(tile_cells, dtype=jnp.int32)[:, None] == got_cells[None, :]).astype(
        jnp.bfloat16
    )
    assimilated = jnp.dot(cell_match, slot_embedded, preferred_element_type=jnp.float32)
    state = background.reshape(tile_cells, channels).astype(jnp.float32) + assimilated
    state = state.astype(jnp.bfloat16).reshape(height, breadth, channels)
    state_rim = widen(state, 2)
    cotangent_rim = widen(cotangent, 1)
    first_pre = conv_three(state_rim, w_first)
    state_near = state_rim[1:-1, 1:-1].astype(jnp.float32)
    hidden = inside_rows((state_near + activate(first_pre)).astype(jnp.bfloat16))
    hidden_grad = conv_stride_back(cotangent_rim, w_second)
    first_pre_again = lax.optimization_barrier(first_pre)
    first_grad = inside_rows(activate_back(first_pre_again, hidden_grad).astype(jnp.bfloat16))
    state_grad = hidden_grad[1:-1, 1:-1] + conv_three_back(first_grad, w_first)
    state_grad = state_grad.astype(jnp.bfloat16).reshape(tile_cells, channels)
    arrived_grad = lax.dot_general(
        cell_match, state_grad, (((0,), (0,)), ((), ())), preferred_element_type=jnp.float32
    )
    slot_back = activate_back(slot_pre, arrived_grad).astype(jnp.bfloat16)
    slot_grad = lax.dot_general(
        slot_back, w_station, (((1,), (1,)), ((), ())), preferred_element_type=jnp.float32
    ).astype(jnp.bfloat16)
    weight_term = lax.dot_general(
        got_obs, slot_back, (((0,), (0,)), ((), ())), preferred_element_type=jnp.float32
    )
    hidden, slot_grad = lax.optimization_barrier((hidden, slot_grad))
    returned = send_back(slot_grad, lon_count, lat_count, capacity)
    encoded = conv_stride(hidden, w_second).astype(jnp.bfloat16)
    returned, weight_term = lax.optimization_barrier((returned, weight_term))
    station_grad = lax.dot_general(
        slot_pick, returned, (((0,), (0,)), ((), ())), preferred_element_type=jnp.float32
    ).astype(jnp.bfloat16)
    weight_grad = sum_over_devices(weight_term, tile_count)
    weight_grad = weight_grad * (1.0 / math.sqrt(station_count * tile_count))
    return (encoded, station_grad, weight_grad)


def solution(mesh):
    in_specs = (
        P("lat", "lon", None),
        P(("lon", "lat"), None),
        P(),
        P(),
        P(),
        P("lat", "lon", None),
        P(("lon", "lat"), None),
        P(("lon", "lat")),
    )
    out_specs = (P("lat", "lon", None), P(("lon", "lat"), None), P())
    return jax.shard_map(
        on_device, mesh=mesh, in_specs=in_specs, out_specs=out_specs, check_vma=False
    )
```

```python
import math

import jax
import jax.numpy as jnp
from jax import lax
from jax.sharding import PartitionSpec as P

def padded_2(cells, sides, width, closed):
    for axis, dim in sides:
        count = lax.axis_size(axis)
        ends = count if closed else count - 1
        head = lax.slice_in_dim(cells, 0, width, axis=dim)
        tail = lax.slice_in_dim(cells, cells.shape[dim] - width, cells.shape[dim], axis=dim)
        cells = jnp.concatenate(
            [
                lax.ppermute(tail, axis, [(i, (i + 1) % count) for i in range(ends)]),
                cells,
                lax.ppermute(head, axis, [((i + 1) % count, i) for i in range(ends)]),
            ],
            axis=dim,
        )
    return cells


def activate(values):
    return jax.nn.gelu(values, approximate=True)


def activate_back(values, upstream):
    return jax.vjp(activate, values)[1](upstream)[0]


def widen(grid_field, width):
    lon_sides = padded_2(grid_field, (("lon", 1),), width, True)
    return padded_2(lon_sides, (("lat", 0),), width, False)


def widen_at_once(cells, width):
    lons = lax.axis_size("lon")
    lats = lax.axis_size("lat")
    both = ("lon", "lat")

    def at(lon, lat):
        return (lon % lons) * lats + lat

    def along_lon(part, step):
        return lax.ppermute(part, "lon", [(i, (i + step) % lons) for i in range(lons)])

    def along_lat(part, step):
        pairs = [(j, j + step) for j in range(lats) if 0 <= j + step < lats]
        return lax.ppermute(part, "lat", pairs)

    def diagonal(part, lon_step, lat_step):
        pairs = [
            (at(i, j), at(i + lon_step, j + lat_step))
            for i in range(lons)
            for j in range(lats)
            if 0 <= j + lat_step < lats
        ]
        return lax.ppermute(part, both, pairs)

    top, bottom = cells[:width], cells[-width:]
    west = along_lon(cells[:, -width:], 1)
    east = along_lon(cells[:, :width], -1)
    north = along_lat(bottom, 1)
    south = along_lat(top, -1)
    north_west = diagonal(bottom[:, -width:], 1, 1)
    north_east = diagonal(bottom[:, :width], -1, 1)
    south_west = diagonal(top[:, -width:], 1, -1)
    south_east = diagonal(top[:, :width], -1, -1)
    return jnp.concatenate(
        [
            jnp.concatenate([north_west, north, north_east], axis=1),
            jnp.concatenate([west, cells, east], axis=1),
            jnp.concatenate([south_west, south, south_east], axis=1),
        ],
        axis=0,
    )


def inside_rows(field):
    lat_index = lax.axis_index("lat")
    last = lax.axis_size("lat") - 1
    rows = jnp.arange(field.shape[0])[:, None, None]
    outside = ((rows == 0) & (lat_index == 0)) | ((rows == field.shape[0] - 1) & (lat_index == last))
    return jnp.where(outside, jnp.zeros_like(field), field)


def conv_valid(padded, kernel, stride, dilation, spec, rim=0):
    result = lax.conv_general_dilated(
        padded[None],
        kernel,
        (stride, stride),
        ((rim, rim), (rim, rim)),
        lhs_dilation=(dilation, dilation),
        dimension_numbers=("NHWC", spec, "NHWC"),
        preferred_element_type=jnp.float32,
    )
    return result[0]


def conv_three(padded, weight):
    return conv_valid(padded, weight, 1, 1, "HWIO")


def conv_stride(padded, weight):
    return conv_valid(padded, weight, 2, 1, "HWIO")


def conv_three_back(extended, weight):
    return conv_valid(extended, weight[::-1, ::-1], 1, 1, "HWOI")


def conv_stride_back(extended, weight):
    return conv_valid(extended, weight[::-1, ::-1], 1, 2, "HWOI", 1)


def send_out(payload, cell_ids, lon_count, lat_count, capacity):
    feature_width = payload.shape[1]
    got_load, got_cells = (
        lax.all_to_all(
            payload.reshape(lon_count * lat_count, capacity, feature_width),
            ("lon", "lat"),
            split_axis=0,
            concat_axis=0,
            tiled=True,
        ),
        lax.all_to_all(
            cell_ids.reshape(lon_count * lat_count, capacity),
            ("lon", "lat"),
            split_axis=0,
            concat_axis=0,
            tiled=True,
        ),
    )
    return (got_load.reshape(-1, feature_width), got_cells.reshape(-1))


def send_back(reply_rows, lon_count, lat_count, capacity):
    feature_width = reply_rows.shape[1]
    returned = lax.all_to_all(
        reply_rows.reshape(lon_count * lat_count, capacity, feature_width),
        ("lon", "lat"),
        split_axis=0,
        concat_axis=0,
        tiled=True,
    )
    return returned.reshape(-1, feature_width)


def sum_over_devices(term, count):
    rows, width = term.shape
    if rows % count != 0:
        return lax.psum(term, ("lon", "lat"))
    pieces = term.reshape(count, rows // count, width)
    gathered = lax.all_to_all(pieces, ("lon", "lat"), split_axis=0, concat_axis=0, tiled=True)
    own = jnp.sum(gathered, axis=0, keepdims=True)
    spread = jnp.broadcast_to(own, (count, rows // count, width))
    whole = lax.all_to_all(spread, ("lon", "lat"), split_axis=0, concat_axis=0, tiled=True)
    return whole.reshape(rows, width)


def on_device(
    background, observations, w_station, w_first, w_second, cotangent, station_tile, station_cell
):
    lon_count = lax.axis_size("lon")
    lat_count = lax.axis_size("lat")
    tile_count = lon_count * lat_count
    height, breadth, channels = background.shape
    tile_cells = height * breadth
    station_count = observations.shape[0]
    capacity = 2 * station_count // tile_count
    slot_total = tile_count * capacity
    target_tile = station_tile[:, 0]
    matches = (target_tile[:, None] == jnp.arange(tile_count, dtype=jnp.int32)[None, :]).astype(
        jnp.bfloat16
    )
    order = jnp.arange(station_count, dtype=jnp.int32)
    before = (order[:, None] > order[None, :]).astype(jnp.bfloat16)
    earlier = jnp.dot(before, matches, preferred_element_type=jnp.float32)
    rank = jnp.sum(earlier * matches.astype(jnp.float32), axis=1).astype(jnp.int32)
    flat_slot = target_tile * capacity + rank
    slot_hit = jnp.arange(slot_total, dtype=jnp.int32)[:, None] == flat_slot[None, :]
    slot_pick = slot_hit.astype(jnp.bfloat16)
    send_cells = jnp.sum(jnp.where(slot_hit, station_cell[None, :] + 1, 0), axis=1) - 1
    send_rows = jnp.dot(slot_pick, observations, preferred_element_type=jnp.float32).astype(
        jnp.bfloat16
    )
    got_obs, got_cells = send_out(send_rows, send_cells, lon_count, lat_count, capacity)
    slot_pre = jnp.dot(got_obs, w_station, preferred_element_type=jnp.float32)
    slot_embedded = activate(slot_pre).astype(jnp.bfloat16)
    cell_match = (jnp.arange(tile_cells, dtype=jnp.int32)[:, None] == got_cells[None, :]).astype(
        jnp.bfloat16
    )
    assimilated = jnp.dot(cell_match, slot_embedded, preferred_element_type=jnp.float32)
    state = background.reshape(tile_cells, channels).astype(jnp.float32) + assimilated
    state = state.astype(jnp.bfloat16).reshape(height, breadth, channels)
    state_rim = widen_at_once(state, 2)
    cotangent_rim = widen(cotangent, 1)
    first_pre = conv_three(state_rim, w_first)
    state_near = state_rim[1:-1, 1:-1].astype(jnp.float32)
    hidden = inside_rows((state_near + activate(first_pre)).astype(jnp.bfloat16))
    encoded = conv_stride(hidden, w_second).astype(jnp.bfloat16)
    hidden_grad = conv_stride_back(cotangent_rim, w_second)
    first_pre_again = lax.optimization_barrier(first_pre)
    first_grad = inside_rows(activate_back(first_pre_again, hidden_grad).astype(jnp.bfloat16))
    state_grad = hidden_grad[1:-1, 1:-1] + conv_three_back(first_grad, w_first)
    state_grad = state_grad.astype(jnp.bfloat16).reshape(tile_cells, channels)
    arrived_grad = lax.dot_general(
        cell_match, state_grad, (((0,), (0,)), ((), ())), preferred_element_type=jnp.float32
    )
    slot_back = activate_back(slot_pre, arrived_grad).astype(jnp.bfloat16)
    slot_grad = lax.dot_general(
        slot_back, w_station, (((1,), (1,)), ((), ())), preferred_element_type=jnp.float32
    ).astype(jnp.bfloat16)
    weight_term = lax.dot_general(
        got_obs, slot_back, (((0,), (0,)), ((), ())), preferred_element_type=jnp.float32
    )
    returned = send_back(slot_grad, lon_count, lat_count, capacity)
    returned, weight_term = lax.optimization_barrier((returned, weight_term))
    station_grad = lax.dot_general(
        slot_pick, returned, (((0,), (0,)), ((), ())), preferred_element_type=jnp.float32
    ).astype(jnp.bfloat16)
    weight_grad = sum_over_devices(weight_term, tile_count)
    weight_grad = weight_grad * (1.0 / math.sqrt(station_count * tile_count))
    return (encoded, station_grad, weight_grad)


def solution(mesh):
    in_specs = (
        P("lat", "lon", None),
        P(("lon", "lat"), None),
        P(),
        P(),
        P(),
        P("lat", "lon", None),
        P(("lon", "lat"), None),
        P(("lon", "lat")),
    )
    out_specs = (P("lat", "lon", None), P(("lon", "lat"), None), P())
    return jax.shard_map(
        on_device, mesh=mesh, in_specs=in_specs, out_specs=out_specs, check_vma=False
    )
```

```python
import math

import jax
import jax.numpy as jnp
from jax import lax
from jax.sharding import PartitionSpec as P

def padded_2(cells, sides, width, closed):
    for axis, dim in sides:
        count = lax.axis_size(axis)
        ends = count if closed else count - 1
        head = lax.slice_in_dim(cells, 0, width, axis=dim)
        tail = lax.slice_in_dim(cells, cells.shape[dim] - width, cells.shape[dim], axis=dim)
        cells = jnp.concatenate(
            [
                lax.ppermute(tail, axis, [(i, (i + 1) % count) for i in range(ends)]),
                cells,
                lax.ppermute(head, axis, [((i + 1) % count, i) for i in range(ends)]),
            ],
            axis=dim,
        )
    return cells


def activate(values):
    return jax.nn.gelu(values, approximate=True)


def activate_back(values, upstream):
    return jax.vjp(activate, values)[1](upstream)[0]


def widen(grid_field, width):
    lon_sides = padded_2(grid_field, (("lon", 1),), width, True)
    return padded_2(lon_sides, (("lat", 0),), width, False)


def inside_rows(field):
    lat_index = lax.axis_index("lat")
    last = lax.axis_size("lat") - 1
    rows = jnp.arange(field.shape[0])[:, None, None]
    outside = ((rows == 0) & (lat_index == 0)) | ((rows == field.shape[0] - 1) & (lat_index == last))
    return jnp.where(outside, jnp.zeros_like(field), field)


def conv_valid(padded, kernel, stride, dilation, spec, rim=0):
    result = lax.conv_general_dilated(
        padded[None],
        kernel,
        (stride, stride),
        ((rim, rim), (rim, rim)),
        lhs_dilation=(dilation, dilation),
        dimension_numbers=("NHWC", spec, "NHWC"),
        preferred_element_type=jnp.float32,
    )
    return result[0]


def conv_three(padded, weight):
    return conv_valid(padded, weight, 1, 1, "HWIO")


def conv_stride(padded, weight):
    return conv_valid(padded, weight, 2, 1, "HWIO")


def conv_three_back(extended, weight):
    return conv_valid(extended, weight[::-1, ::-1], 1, 1, "HWOI")


def conv_stride_back(extended, weight):
    return conv_valid(extended, weight[::-1, ::-1], 1, 2, "HWOI", 1)


def send_out(payload, cell_ids, lon_count, lat_count, capacity):
    feature_width = payload.shape[1]
    got_load, got_cells = (
        lax.all_to_all(
            payload.reshape(lon_count * lat_count, capacity, feature_width),
            ("lon", "lat"),
            split_axis=0,
            concat_axis=0,
            tiled=True,
        ),
        lax.all_to_all(
            cell_ids.reshape(lon_count * lat_count, capacity),
            ("lon", "lat"),
            split_axis=0,
            concat_axis=0,
            tiled=True,
        ),
    )
    return (got_load.reshape(-1, feature_width), got_cells.reshape(-1))


def send_back(reply_rows, lon_count, lat_count, capacity):
    feature_width = reply_rows.shape[1]
    returned = lax.all_to_all(
        reply_rows.reshape(lon_count * lat_count, capacity, feature_width),
        ("lon", "lat"),
        split_axis=0,
        concat_axis=0,
        tiled=True,
    )
    return returned.reshape(-1, feature_width)


def split_rows(term, count):
    rows, width = term.shape
    if rows % count != 0:
        return term
    return term.reshape(count, rows // count, width)


def sum_over_devices(pieces, count):
    if pieces.ndim == 2:
        return lax.psum(pieces, ("lon", "lat"))
    rows, width = pieces.shape[0] * pieces.shape[1], pieces.shape[2]
    gathered = lax.all_to_all(pieces, ("lon", "lat"), split_axis=0, concat_axis=0, tiled=True)
    own = jnp.sum(gathered, axis=0, keepdims=True)
    spread = jnp.broadcast_to(own, (count, rows // count, width))
    whole = lax.all_to_all(spread, ("lon", "lat"), split_axis=0, concat_axis=0, tiled=True)
    return whole.reshape(rows, width)


def on_device(
    background, observations, w_station, w_first, w_second, cotangent, station_tile, station_cell
):
    lon_count = lax.axis_size("lon")
    lat_count = lax.axis_size("lat")
    tile_count = lon_count * lat_count
    height, breadth, channels = background.shape
    tile_cells = height * breadth
    station_count = observations.shape[0]
    capacity = 2 * station_count // tile_count
    slot_total = tile_count * capacity
    target_tile = station_tile[:, 0]
    matches = (target_tile[:, None] == jnp.arange(tile_count, dtype=jnp.int32)[None, :]).astype(
        jnp.bfloat16
    )
    order = jnp.arange(station_count, dtype=jnp.int32)
    before = (order[:, None] > order[None, :]).astype(jnp.bfloat16)
    earlier = jnp.dot(before, matches, preferred_element_type=jnp.float32)
    rank = jnp.sum(earlier * matches.astype(jnp.float32), axis=1).astype(jnp.int32)
    flat_slot = target_tile * capacity + rank
    slot_hit = jnp.arange(slot_total, dtype=jnp.int32)[:, None] == flat_slot[None, :]
    slot_pick = slot_hit.astype(jnp.bfloat16)
    send_cells = jnp.sum(jnp.where(slot_hit, station_cell[None, :] + 1, 0), axis=1) - 1
    send_rows = jnp.dot(slot_pick, observations, preferred_element_type=jnp.float32).astype(
        jnp.bfloat16
    )
    got_obs, got_cells = send_out(send_rows, send_cells, lon_count, lat_count, capacity)
    slot_pre = jnp.dot(got_obs, w_station, preferred_element_type=jnp.float32)
    slot_embedded = activate(slot_pre).astype(jnp.bfloat16)
    cell_match = (jnp.arange(tile_cells, dtype=jnp.int32)[:, None] == got_cells[None, :]).astype(
        jnp.bfloat16
    )
    assimilated = jnp.dot(cell_match, slot_embedded, preferred_element_type=jnp.float32)
    state = background.reshape(tile_cells, channels).astype(jnp.float32) + assimilated
    state = state.astype(jnp.bfloat16).reshape(height, breadth, channels)
    state_rim = widen(state, 2)
    cotangent_rim = widen(cotangent, 1)
    first_pre = conv_three(state_rim, w_first)
    state_near = state_rim[1:-1, 1:-1].astype(jnp.float32)
    hidden = inside_rows((state_near + activate(first_pre)).astype(jnp.bfloat16))
    encoded = conv_stride(hidden, w_second).astype(jnp.bfloat16)
    hidden_grad = conv_stride_back(cotangent_rim, w_second)
    first_pre_again = lax.optimization_barrier(first_pre)
    first_grad = inside_rows(activate_back(first_pre_again, hidden_grad).astype(jnp.bfloat16))
    state_grad = hidden_grad[1:-1, 1:-1] + conv_three_back(first_grad, w_first)
    state_grad = state_grad.astype(jnp.bfloat16).reshape(tile_cells, channels)
    arrived_grad = lax.dot_general(
        cell_match, state_grad, (((0,), (0,)), ((), ())), preferred_element_type=jnp.float32
    )
    slot_back = activate_back(slot_pre, arrived_grad).astype(jnp.bfloat16)
    slot_grad = lax.dot_general(
        slot_back, w_station, (((1,), (1,)), ((), ())), preferred_element_type=jnp.float32
    ).astype(jnp.bfloat16)
    weight_term = lax.dot_general(
        got_obs, slot_back, (((0,), (0,)), ((), ())), preferred_element_type=jnp.float32
    )
    returned = send_back(slot_grad, lon_count, lat_count, capacity)
    weight_term = split_rows(weight_term, tile_count)
    returned, weight_term = lax.optimization_barrier((returned, weight_term))
    station_grad = lax.dot_general(
        slot_pick, returned, (((0,), (0,)), ((), ())), preferred_element_type=jnp.float32
    ).astype(jnp.bfloat16)
    weight_grad = sum_over_devices(weight_term, tile_count)
    weight_grad = weight_grad * (1.0 / math.sqrt(station_count * tile_count))
    return (encoded, station_grad, weight_grad)


def solution(mesh):
    in_specs = (
        P("lat", "lon", None),
        P(("lon", "lat"), None),
        P(),
        P(),
        P(),
        P("lat", "lon", None),
        P(("lon", "lat"), None),
        P(("lon", "lat")),
    )
    out_specs = (P("lat", "lon", None), P(("lon", "lat"), None), P())
    return jax.shard_map(
        on_device, mesh=mesh, in_specs=in_specs, out_specs=out_specs, check_vma=False
    )
```

```python
import math

import jax
import jax.numpy as jnp
from jax import lax
from jax.sharding import PartitionSpec as P

def padded_2(cells, sides, width, closed):
    for axis, dim in sides:
        count = lax.axis_size(axis)
        ends = count if closed else count - 1
        head = lax.slice_in_dim(cells, 0, width, axis=dim)
        tail = lax.slice_in_dim(cells, cells.shape[dim] - width, cells.shape[dim], axis=dim)
        cells = jnp.concatenate(
            [
                lax.ppermute(tail, axis, [(i, (i + 1) % count) for i in range(ends)]),
                cells,
                lax.ppermute(head, axis, [((i + 1) % count, i) for i in range(ends)]),
            ],
            axis=dim,
        )
    return cells


def activate(values):
    return jax.nn.gelu(values, approximate=True)


def activate_back(values, upstream):
    return jax.vjp(activate, values)[1](upstream)[0]


def widen(grid_field, width):
    lon_sides = padded_2(grid_field, (("lon", 1),), width, True)
    return padded_2(lon_sides, (("lat", 0),), width, False)


def inside_rows(field):
    lat_index = lax.axis_index("lat")
    last = lax.axis_size("lat") - 1
    rows = jnp.arange(field.shape[0])[:, None, None]
    outside = ((rows == 0) & (lat_index == 0)) | ((rows == field.shape[0] - 1) & (lat_index == last))
    return jnp.where(outside, jnp.zeros_like(field), field)


def conv_valid(padded, kernel, stride, dilation, spec, rim=0):
    result = lax.conv_general_dilated(
        padded[None],
        kernel,
        (stride, stride),
        ((rim, rim), (rim, rim)),
        lhs_dilation=(dilation, dilation),
        dimension_numbers=("NHWC", spec, "NHWC"),
        preferred_element_type=jnp.float32,
    )
    return result[0]


def conv_three(padded, weight):
    return conv_valid(padded, weight, 1, 1, "HWIO")


def conv_stride(padded, weight):
    return conv_valid(padded, weight, 2, 1, "HWIO")


def conv_three_back(extended, weight):
    return conv_valid(extended, weight[::-1, ::-1], 1, 1, "HWOI")


def conv_stride_back(extended, weight):
    return conv_valid(extended, weight[::-1, ::-1], 1, 2, "HWOI", 1)


def send_out(payload, cell_ids, lon_count, lat_count, capacity):
    feature_width = payload.shape[1]
    got_load, got_cells = (
        lax.all_to_all(
            payload.reshape(lon_count * lat_count, capacity, feature_width),
            ("lon", "lat"),
            split_axis=0,
            concat_axis=0,
            tiled=True,
        ),
        lax.all_to_all(
            cell_ids.reshape(lon_count * lat_count, capacity),
            ("lon", "lat"),
            split_axis=0,
            concat_axis=0,
            tiled=True,
        ),
    )
    return (got_load.reshape(-1, feature_width), got_cells.reshape(-1))


def send_back(reply_rows, lon_count, lat_count, capacity):
    feature_width = reply_rows.shape[1]
    returned = lax.all_to_all(
        reply_rows.reshape(lon_count * lat_count, capacity, feature_width),
        ("lon", "lat"),
        split_axis=0,
        concat_axis=0,
        tiled=True,
    )
    return returned.reshape(-1, feature_width)


def sum_over_devices(term, count):
    rows, width = term.shape
    if rows % count != 0:
        return lax.psum(term, ("lon", "lat"))
    pieces = term.reshape(count, rows // count, width)
    gathered = lax.all_to_all(pieces, ("lon", "lat"), split_axis=0, concat_axis=0, tiled=True)
    own = jnp.sum(gathered, axis=0, keepdims=True)
    spread = jnp.broadcast_to(own, (count, rows // count, width))
    whole = lax.all_to_all(spread, ("lon", "lat"), split_axis=0, concat_axis=0, tiled=True)
    return whole.reshape(rows, width)


def on_device(
    background, observations, w_station, w_first, w_second, cotangent, station_tile, station_cell
):
    lon_count = lax.axis_size("lon")
    lat_count = lax.axis_size("lat")
    tile_count = lon_count * lat_count
    height, breadth, channels = background.shape
    tile_cells = height * breadth
    station_count = observations.shape[0]
    capacity = 2 * station_count // tile_count
    slot_total = tile_count * capacity
    target_tile = station_tile[:, 0]
    matches = (target_tile[:, None] == jnp.arange(tile_count, dtype=jnp.int32)[None, :]).astype(
        jnp.bfloat16
    )
    order = jnp.arange(station_count, dtype=jnp.int32)
    before = (order[:, None] > order[None, :]).astype(jnp.bfloat16)
    earlier = jnp.dot(before, matches, preferred_element_type=jnp.float32)
    rank = jnp.sum(earlier * matches.astype(jnp.float32), axis=1).astype(jnp.int32)
    flat_slot = target_tile * capacity + rank
    slot_hit = jnp.arange(slot_total, dtype=jnp.int32)[:, None] == flat_slot[None, :]
    slot_pick = slot_hit.astype(jnp.bfloat16)
    send_cells = jnp.sum(jnp.where(slot_hit, station_cell[None, :] + 1, 0), axis=1) - 1
    send_rows = jnp.dot(slot_pick, observations, preferred_element_type=jnp.float32).astype(
        jnp.bfloat16
    )
    got_obs, got_cells = send_out(send_rows, send_cells, lon_count, lat_count, capacity)
    slot_pre = jnp.dot(got_obs, w_station, preferred_element_type=jnp.float32)
    slot_embedded = activate(slot_pre).astype(jnp.bfloat16)
    cell_match = (jnp.arange(tile_cells, dtype=jnp.int32)[:, None] == got_cells[None, :]).astype(
        jnp.bfloat16
    )
    assimilated = jnp.dot(cell_match, slot_embedded, preferred_element_type=jnp.float32)
    state = background.reshape(tile_cells, channels).astype(jnp.float32) + assimilated
    state = state.astype(jnp.bfloat16).reshape(height, breadth, channels)
    cotangent_lon = padded_2(cotangent, (("lon", 1),), 1, True)
    state_rim = widen(state, 2)
    cotangent_lon, state_rim = lax.optimization_barrier((cotangent_lon, state_rim))
    cotangent_rim = padded_2(cotangent_lon, (("lat", 0),), 1, False)
    first_pre = conv_three(state_rim, w_first)
    state_near = state_rim[1:-1, 1:-1].astype(jnp.float32)
    hidden = inside_rows((state_near + activate(first_pre)).astype(jnp.bfloat16))
    encoded = conv_stride(hidden, w_second).astype(jnp.bfloat16)
    hidden_grad = conv_stride_back(cotangent_rim, w_second)
    first_pre_again = lax.optimization_barrier(first_pre)
    first_grad = inside_rows(activate_back(first_pre_again, hidden_grad).astype(jnp.bfloat16))
    state_grad = hidden_grad[1:-1, 1:-1] + conv_three_back(first_grad, w_first)
    state_grad = state_grad.astype(jnp.bfloat16).reshape(tile_cells, channels)
    arrived_grad = lax.dot_general(
        cell_match, state_grad, (((0,), (0,)), ((), ())), preferred_element_type=jnp.float32
    )
    slot_back = activate_back(slot_pre, arrived_grad).astype(jnp.bfloat16)
    slot_grad = lax.dot_general(
        slot_back, w_station, (((1,), (1,)), ((), ())), preferred_element_type=jnp.float32
    ).astype(jnp.bfloat16)
    weight_term = lax.dot_general(
        got_obs, slot_back, (((0,), (0,)), ((), ())), preferred_element_type=jnp.float32
    )
    returned = send_back(slot_grad, lon_count, lat_count, capacity)
    returned, weight_term = lax.optimization_barrier((returned, weight_term))
    station_grad = lax.dot_general(
        slot_pick, returned, (((0,), (0,)), ((), ())), preferred_element_type=jnp.float32
    ).astype(jnp.bfloat16)
    weight_grad = sum_over_devices(weight_term, tile_count)
    weight_grad = weight_grad * (1.0 / math.sqrt(station_count * tile_count))
    return (encoded, station_grad, weight_grad)


def solution(mesh):
    in_specs = (
        P("lat", "lon", None),
        P(("lon", "lat"), None),
        P(),
        P(),
        P(),
        P("lat", "lon", None),
        P(("lon", "lat"), None),
        P(("lon", "lat")),
    )
    out_specs = (P("lat", "lon", None), P(("lon", "lat"), None), P())
    return jax.shard_map(
        on_device, mesh=mesh, in_specs=in_specs, out_specs=out_specs, check_vma=False
    )
```

```python
import math

import jax
import jax.numpy as jnp
from jax import lax
from jax.sharding import PartitionSpec as P

def padded_2(cells, sides, width, closed):
    for axis, dim in sides:
        count = lax.axis_size(axis)
        ends = count if closed else count - 1
        head = lax.slice_in_dim(cells, 0, width, axis=dim)
        tail = lax.slice_in_dim(cells, cells.shape[dim] - width, cells.shape[dim], axis=dim)
        cells = jnp.concatenate(
            [
                lax.ppermute(tail, axis, [(i, (i + 1) % count) for i in range(ends)]),
                cells,
                lax.ppermute(head, axis, [((i + 1) % count, i) for i in range(ends)]),
            ],
            axis=dim,
        )
    return cells


def activate(values):
    return jax.nn.gelu(values, approximate=True)


def activate_back(values, upstream):
    return jax.vjp(activate, values)[1](upstream)[0]


def widen(grid_field, width):
    lon_sides = padded_2(grid_field, (("lon", 1),), width, True)
    return padded_2(lon_sides, (("lat", 0),), width, False)


def inside_rows(field):
    lat_index = lax.axis_index("lat")
    last = lax.axis_size("lat") - 1
    rows = jnp.arange(field.shape[0])[:, None, None]
    outside = ((rows == 0) & (lat_index == 0)) | ((rows == field.shape[0] - 1) & (lat_index == last))
    return jnp.where(outside, jnp.zeros_like(field), field)


def conv_valid(padded, kernel, stride, dilation, spec, rim=0):
    result = lax.conv_general_dilated(
        padded[None],
        kernel,
        (stride, stride),
        ((rim, rim), (rim, rim)),
        lhs_dilation=(dilation, dilation),
        dimension_numbers=("NHWC", spec, "NHWC"),
        preferred_element_type=jnp.float32,
    )
    return result[0]


def conv_three(padded, weight):
    return conv_valid(padded, weight, 1, 1, "HWIO")


def conv_stride(padded, weight):
    return conv_valid(padded, weight, 2, 1, "HWIO")


def conv_three_back(extended, weight):
    return conv_valid(extended, weight[::-1, ::-1], 1, 1, "HWOI")


def conv_stride_back(extended, weight):
    return conv_valid(extended, weight[::-1, ::-1], 1, 2, "HWOI", 1)


def send_out(payload, cell_ids, lon_count, lat_count, capacity):
    feature_width = payload.shape[1]
    got_load, got_cells = (
        lax.all_to_all(
            payload.reshape(lon_count * lat_count, capacity, feature_width),
            ("lon", "lat"),
            split_axis=0,
            concat_axis=0,
            tiled=True,
        ),
        lax.all_to_all(
            cell_ids.reshape(lon_count * lat_count, capacity),
            ("lon", "lat"),
            split_axis=0,
            concat_axis=0,
            tiled=True,
        ),
    )
    return (got_load.reshape(-1, feature_width), got_cells.reshape(-1))


def send_back(reply_rows, lon_count, lat_count, capacity):
    feature_width = reply_rows.shape[1]
    returned = lax.all_to_all(
        reply_rows.reshape(lon_count * lat_count, capacity, feature_width),
        ("lon", "lat"),
        split_axis=0,
        concat_axis=0,
        tiled=True,
    )
    return returned.reshape(-1, feature_width)


def sum_over_devices(term, count, scale):
    rows, width = term.shape
    if rows % count != 0:
        return lax.psum(term, ("lon", "lat")) * scale
    pieces = term.reshape(count, rows // count, width)
    gathered = lax.all_to_all(pieces, ("lon", "lat"), split_axis=0, concat_axis=0, tiled=True)
    own = jnp.sum(gathered, axis=0, keepdims=True) * scale
    spread = jnp.broadcast_to(own, (count, rows // count, width))
    whole = lax.all_to_all(spread, ("lon", "lat"), split_axis=0, concat_axis=0, tiled=True)
    return whole.reshape(rows, width)


def on_device(
    background, observations, w_station, w_first, w_second, cotangent, station_tile, station_cell
):
    lon_count = lax.axis_size("lon")
    lat_count = lax.axis_size("lat")
    tile_count = lon_count * lat_count
    height, breadth, channels = background.shape
    tile_cells = height * breadth
    station_count = observations.shape[0]
    capacity = 2 * station_count // tile_count
    slot_total = tile_count * capacity
    target_tile = station_tile[:, 0]
    matches = (target_tile[:, None] == jnp.arange(tile_count, dtype=jnp.int32)[None, :]).astype(
        jnp.bfloat16
    )
    order = jnp.arange(station_count, dtype=jnp.int32)
    before = (order[:, None] > order[None, :]).astype(jnp.bfloat16)
    earlier = jnp.dot(before, matches, preferred_element_type=jnp.float32)
    rank = jnp.sum(earlier * matches.astype(jnp.float32), axis=1).astype(jnp.int32)
    flat_slot = target_tile * capacity + rank
    slot_hit = jnp.arange(slot_total, dtype=jnp.int32)[:, None] == flat_slot[None, :]
    slot_pick = slot_hit.astype(jnp.bfloat16)
    send_cells = jnp.sum(jnp.where(slot_hit, station_cell[None, :] + 1, 0), axis=1) - 1
    send_rows = jnp.dot(slot_pick, observations, preferred_element_type=jnp.float32).astype(
        jnp.bfloat16
    )
    got_obs, got_cells = send_out(send_rows, send_cells, lon_count, lat_count, capacity)
    slot_pre = jnp.dot(got_obs, w_station, preferred_element_type=jnp.float32)
    slot_embedded = activate(slot_pre).astype(jnp.bfloat16)
    cell_match = (jnp.arange(tile_cells, dtype=jnp.int32)[:, None] == got_cells[None, :]).astype(
        jnp.bfloat16
    )
    assimilated = jnp.dot(cell_match, slot_embedded, preferred_element_type=jnp.float32)
    state = background.reshape(tile_cells, channels).astype(jnp.float32) + assimilated
    state = state.astype(jnp.bfloat16).reshape(height, breadth, channels)
    state_rim = widen(state, 2)
    cotangent_rim = widen(cotangent, 1)
    first_pre = conv_three(state_rim, w_first)
    state_near = state_rim[1:-1, 1:-1].astype(jnp.float32)
    hidden = inside_rows((state_near + activate(first_pre)).astype(jnp.bfloat16))
    encoded = conv_stride(hidden, w_second).astype(jnp.bfloat16)
    hidden_grad = conv_stride_back(cotangent_rim, w_second)
    first_pre_again = lax.optimization_barrier(first_pre)
    first_grad = inside_rows(activate_back(first_pre_again, hidden_grad).astype(jnp.bfloat16))
    state_grad = hidden_grad[1:-1, 1:-1] + conv_three_back(first_grad, w_first)
    state_grad = state_grad.astype(jnp.bfloat16).reshape(tile_cells, channels)
    arrived_grad = lax.dot_general(
        cell_match, state_grad, (((0,), (0,)), ((), ())), preferred_element_type=jnp.float32
    )
    slot_back = activate_back(slot_pre, arrived_grad).astype(jnp.bfloat16)
    slot_grad = lax.dot_general(
        slot_back, w_station, (((1,), (1,)), ((), ())), preferred_element_type=jnp.float32
    ).astype(jnp.bfloat16)
    weight_term = lax.dot_general(
        got_obs, slot_back, (((0,), (0,)), ((), ())), preferred_element_type=jnp.float32
    )
    returned = send_back(slot_grad, lon_count, lat_count, capacity)
    returned, weight_term = lax.optimization_barrier((returned, weight_term))
    station_grad = lax.dot_general(
        slot_pick, returned, (((0,), (0,)), ((), ())), preferred_element_type=jnp.float32
    ).astype(jnp.bfloat16)
    weight_grad = sum_over_devices(
        weight_term, tile_count, 1.0 / math.sqrt(station_count * tile_count)
    )
    return (encoded, station_grad, weight_grad)


def solution(mesh):
    in_specs = (
        P("lat", "lon", None),
        P(("lon", "lat"), None),
        P(),
        P(),
        P(),
        P("lat", "lon", None),
        P(("lon", "lat"), None),
        P(("lon", "lat")),
    )
    out_specs = (P("lat", "lon", None), P(("lon", "lat"), None), P())
    return jax.shard_map(
        on_device, mesh=mesh, in_specs=in_specs, out_specs=out_specs, check_vma=False
    )
```

```python
import math

import jax
import jax.numpy as jnp
from jax import lax
from jax.sharding import PartitionSpec as P

def padded_2(cells, sides, width, closed):
    for axis, dim in sides:
        count = lax.axis_size(axis)
        ends = count if closed else count - 1
        head = lax.slice_in_dim(cells, 0, width, axis=dim)
        tail = lax.slice_in_dim(cells, cells.shape[dim] - width, cells.shape[dim], axis=dim)
        cells = jnp.concatenate(
            [
                lax.ppermute(tail, axis, [(i, (i + 1) % count) for i in range(ends)]),
                cells,
                lax.ppermute(head, axis, [((i + 1) % count, i) for i in range(ends)]),
            ],
            axis=dim,
        )
    return cells


def activate(values):
    return jax.nn.gelu(values, approximate=True)


def activate_back(values, upstream):
    return jax.vjp(activate, values)[1](upstream)[0]


def widen(grid_field, width):
    lon_sides = padded_2(grid_field, (("lon", 1),), width, True)
    return padded_2(lon_sides, (("lat", 0),), width, False)


def inside_rows(field):
    lat_index = lax.axis_index("lat")
    last = lax.axis_size("lat") - 1
    rows = jnp.arange(field.shape[0])[:, None, None]
    outside = ((rows == 0) & (lat_index == 0)) | ((rows == field.shape[0] - 1) & (lat_index == last))
    return jnp.where(outside, jnp.zeros_like(field), field)


def conv_valid(padded, kernel, stride, dilation, spec, rim=0):
    result = lax.conv_general_dilated(
        padded[None],
        kernel,
        (stride, stride),
        ((rim, rim), (rim, rim)),
        lhs_dilation=(dilation, dilation),
        dimension_numbers=("NHWC", spec, "NHWC"),
        preferred_element_type=jnp.float32,
    )
    return result[0]


def conv_three(padded, weight):
    return conv_valid(padded, weight, 1, 1, "HWIO")


def conv_stride(padded, weight):
    return conv_valid(padded, weight, 2, 1, "HWIO")


def conv_three_back(extended, weight):
    return conv_valid(extended, weight[::-1, ::-1], 1, 1, "HWOI")


def conv_stride_back(extended, weight):
    return conv_valid(extended, weight[::-1, ::-1], 1, 2, "HWOI", 1)


def send_out(payload, cell_ids, lon_count, lat_count, capacity):
    feature_width = payload.shape[1]
    got_load, got_cells = (
        lax.all_to_all(
            payload.reshape(lon_count * lat_count, capacity, feature_width),
            ("lon", "lat"),
            split_axis=0,
            concat_axis=0,
            tiled=True,
        ),
        lax.all_to_all(
            cell_ids.reshape(lon_count * lat_count, capacity),
            ("lon", "lat"),
            split_axis=0,
            concat_axis=0,
            tiled=True,
        ),
    )
    return (got_load.reshape(-1, feature_width), got_cells.reshape(-1))


def send_back(reply_rows, lon_count, lat_count, capacity):
    feature_width = reply_rows.shape[1]
    returned = lax.all_to_all(
        reply_rows.reshape(lon_count * lat_count, capacity, feature_width),
        ("lon", "lat"),
        split_axis=0,
        concat_axis=0,
        tiled=True,
    )
    return returned.reshape(-1, feature_width)


def sum_over_devices(term, count):
    rows, width = term.shape
    if rows % count != 0:
        return lax.psum(term, ("lon", "lat"))
    pieces = term.reshape(count, rows // count, width)
    gathered = lax.all_to_all(pieces, ("lon", "lat"), split_axis=0, concat_axis=0, tiled=True)
    own = jnp.sum(gathered, axis=0, keepdims=True)
    spread = jnp.broadcast_to(own, (count, rows // count, width))
    whole = lax.all_to_all(spread, ("lon", "lat"), split_axis=0, concat_axis=0, tiled=True)
    return whole.reshape(rows, width)


def on_device(
    background, observations, w_station, w_first, w_second, cotangent, station_tile, station_cell
):
    lon_count = lax.axis_size("lon")
    lat_count = lax.axis_size("lat")
    tile_count = lon_count * lat_count
    height, breadth, channels = background.shape
    tile_cells = height * breadth
    station_count = observations.shape[0]
    capacity = 2 * station_count // tile_count
    slot_total = tile_count * capacity
    target_tile = station_tile[:, 0]
    matches = (target_tile[:, None] == jnp.arange(tile_count, dtype=jnp.int32)[None, :]).astype(
        jnp.bfloat16
    )
    order = jnp.arange(station_count, dtype=jnp.int32)
    before = (order[:, None] > order[None, :]).astype(jnp.bfloat16)
    earlier = jnp.dot(before, matches, preferred_element_type=jnp.float32)
    rank = jnp.sum(earlier * matches.astype(jnp.float32), axis=1).astype(jnp.int32)
    flat_slot = target_tile * capacity + rank
    slot_hit = jnp.arange(slot_total, dtype=jnp.int32)[:, None] == flat_slot[None, :]
    slot_pick = slot_hit.astype(jnp.bfloat16)
    send_cells = jnp.sum(jnp.where(slot_hit, station_cell[None, :] + 1, 0), axis=1) - 1
    send_rows = jnp.dot(slot_pick, observations, preferred_element_type=jnp.float32).astype(
        jnp.bfloat16
    )
    got_obs, got_cells = send_out(send_rows, send_cells, lon_count, lat_count, capacity)
    slot_pre = jnp.dot(got_obs, w_station, preferred_element_type=jnp.float32)
    slot_embedded = activate(slot_pre).astype(jnp.bfloat16)
    cell_match = (jnp.arange(tile_cells, dtype=jnp.int32)[:, None] == got_cells[None, :]).astype(
        jnp.bfloat16
    )
    assimilated = jnp.dot(cell_match, slot_embedded, preferred_element_type=jnp.float32)
    state = background.reshape(tile_cells, channels).astype(jnp.float32) + assimilated
    state = state.astype(jnp.bfloat16).reshape(height, breadth, channels)
    state_rim = widen(state, 2)
    cotangent_rim = widen(cotangent, 1)
    first_pre = conv_three(state_rim, w_first)
    state_near = state_rim[1:-1, 1:-1].astype(jnp.float32)
    hidden = inside_rows((state_near + activate(first_pre)).astype(jnp.bfloat16))
    encoded = conv_stride(hidden, w_second).astype(jnp.bfloat16)
    hidden_grad = conv_stride_back(cotangent_rim, w_second)
    first_pre_again = lax.optimization_barrier(first_pre)
    first_grad = inside_rows(activate_back(first_pre_again, hidden_grad).astype(jnp.bfloat16))
    state_grad = hidden_grad[1:-1, 1:-1] + conv_three_back(first_grad, w_first)
    state_grad = state_grad.astype(jnp.bfloat16).reshape(tile_cells, channels)
    parts = 2 if capacity % 2 == 0 else 1
    share = capacity // parts
    weight_term = None
    returned_parts = []
    for part in range(parts):
        part_cells = got_cells.reshape(tile_count, parts, share)[:, part].reshape(-1)
        part_obs = got_obs.reshape(tile_count, parts, share, -1)[:, part].reshape(
            tile_count * share, -1
        )
        part_pre = slot_pre.reshape(tile_count, parts, share, -1)[:, part].reshape(
            tile_count * share, -1
        )
        part_match = (
            jnp.arange(tile_cells, dtype=jnp.int32)[:, None] == part_cells[None, :]
        ).astype(jnp.bfloat16)
        arrived_grad = lax.dot_general(
            part_match, state_grad, (((0,), (0,)), ((), ())), preferred_element_type=jnp.float32
        )
        slot_back = activate_back(part_pre, arrived_grad).astype(jnp.bfloat16)
        slot_grad = lax.dot_general(
            slot_back, w_station, (((1,), (1,)), ((), ())), preferred_element_type=jnp.float32
        ).astype(jnp.bfloat16)
        part_term = lax.dot_general(
            part_obs, slot_back, (((0,), (0,)), ((), ())), preferred_element_type=jnp.float32
        )
        weight_term = part_term if weight_term is None else weight_term + part_term
        returned_parts.append(send_back(slot_grad, lon_count, lat_count, share))
    returned = jnp.stack(
        [r.reshape(tile_count, share, -1) for r in returned_parts], axis=1
    ).reshape(slot_total, -1)
    returned, weight_term = lax.optimization_barrier((returned, weight_term))
    station_grad = lax.dot_general(
        slot_pick, returned, (((0,), (0,)), ((), ())), preferred_element_type=jnp.float32
    ).astype(jnp.bfloat16)
    weight_grad = sum_over_devices(weight_term, tile_count)
    weight_grad = weight_grad * (1.0 / math.sqrt(station_count * tile_count))
    return (encoded, station_grad, weight_grad)


def solution(mesh):
    in_specs = (
        P("lat", "lon", None),
        P(("lon", "lat"), None),
        P(),
        P(),
        P(),
        P("lat", "lon", None),
        P(("lon", "lat"), None),
        P(("lon", "lat")),
    )
    out_specs = (P("lat", "lon", None), P(("lon", "lat"), None), P())
    return jax.shard_map(
        on_device, mesh=mesh, in_specs=in_specs, out_specs=out_specs, check_vma=False
    )
```

```python
import math

import jax
import jax.numpy as jnp
from jax import lax
from jax.sharding import PartitionSpec as P

def padded_2(cells, sides, width, closed):
    for axis, dim in sides:
        count = lax.axis_size(axis)
        ends = count if closed else count - 1
        head = lax.slice_in_dim(cells, 0, width, axis=dim)
        tail = lax.slice_in_dim(cells, cells.shape[dim] - width, cells.shape[dim], axis=dim)
        cells = jnp.concatenate(
            [
                lax.ppermute(tail, axis, [(i, (i + 1) % count) for i in range(ends)]),
                cells,
                lax.ppermute(head, axis, [((i + 1) % count, i) for i in range(ends)]),
            ],
            axis=dim,
        )
    return cells


def activate(values):
    return jax.nn.gelu(values, approximate=True)


def activate_back(values, upstream):
    return jax.vjp(activate, values)[1](upstream)[0]


def widen(grid_field, width):
    lon_sides = padded_2(grid_field, (("lon", 1),), width, True)
    return padded_2(lon_sides, (("lat", 0),), width, False)


def inside_rows(field):
    lat_index = lax.axis_index("lat")
    last = lax.axis_size("lat") - 1
    rows = jnp.arange(field.shape[0])[:, None, None]
    outside = ((rows == 0) & (lat_index == 0)) | ((rows == field.shape[0] - 1) & (lat_index == last))
    return jnp.where(outside, jnp.zeros_like(field), field)


def conv_valid(padded, kernel, stride, dilation, spec, rim=0):
    result = lax.conv_general_dilated(
        padded[None],
        kernel,
        (stride, stride),
        ((rim, rim), (rim, rim)),
        lhs_dilation=(dilation, dilation),
        dimension_numbers=("NHWC", spec, "NHWC"),
        preferred_element_type=jnp.float32,
    )
    return result[0]


def conv_three(padded, weight):
    return conv_valid(padded, weight, 1, 1, "HWIO")


def conv_stride(padded, weight):
    return conv_valid(padded, weight, 2, 1, "HWIO")


def conv_three_back(extended, weight):
    return conv_valid(extended, weight[::-1, ::-1], 1, 1, "HWOI")


def conv_stride_back(extended, weight):
    return conv_valid(extended, weight[::-1, ::-1], 1, 2, "HWOI", 1)


def send_out(payload, cell_ids, lon_count, lat_count, capacity):
    feature_width = payload.shape[1]
    got_load, got_cells = (
        lax.all_to_all(
            payload.reshape(lon_count * lat_count, capacity, feature_width),
            ("lon", "lat"),
            split_axis=0,
            concat_axis=0,
            tiled=True,
        ),
        lax.all_to_all(
            cell_ids.reshape(lon_count * lat_count, capacity),
            ("lon", "lat"),
            split_axis=0,
            concat_axis=0,
            tiled=True,
        ),
    )
    return (got_load.reshape(-1, feature_width), got_cells.reshape(-1))


def send_back(reply_rows, lon_count, lat_count, capacity):
    feature_width = reply_rows.shape[1]
    returned = lax.all_to_all(
        reply_rows.reshape(lon_count * lat_count, capacity, feature_width),
        ("lon", "lat"),
        split_axis=0,
        concat_axis=0,
        tiled=True,
    )
    return returned.reshape(-1, feature_width)


def sum_over_devices(term, count):
    rows, width = term.shape
    if rows % count != 0:
        return lax.psum(term, ("lon", "lat"))
    pieces = term.reshape(count, rows // count, width)
    gathered = lax.all_to_all(pieces, ("lon", "lat"), split_axis=0, concat_axis=0, tiled=True)
    own = jnp.sum(gathered, axis=0, keepdims=True)
    spread = jnp.broadcast_to(own, (count, rows // count, width))
    whole = lax.all_to_all(spread, ("lon", "lat"), split_axis=0, concat_axis=0, tiled=True)
    return whole.reshape(rows, width)


def on_device(
    background, observations, w_station, w_first, w_second, cotangent, station_tile, station_cell
):
    lon_count = lax.axis_size("lon")
    lat_count = lax.axis_size("lat")
    tile_count = lon_count * lat_count
    height, breadth, channels = background.shape
    tile_cells = height * breadth
    station_count = observations.shape[0]
    capacity = 2 * station_count // tile_count
    slot_total = tile_count * capacity
    target_tile = station_tile[:, 0]
    matches = (target_tile[:, None] == jnp.arange(tile_count, dtype=jnp.int32)[None, :]).astype(
        jnp.bfloat16
    )
    order = jnp.arange(station_count, dtype=jnp.int32)
    before = (order[:, None] > order[None, :]).astype(jnp.bfloat16)
    earlier = jnp.dot(before, matches, preferred_element_type=jnp.float32)
    rank = jnp.sum(earlier * matches.astype(jnp.float32), axis=1).astype(jnp.int32)
    flat_slot = target_tile * capacity + rank
    slot_hit = jnp.arange(slot_total, dtype=jnp.int32)[:, None] == flat_slot[None, :]
    slot_pick = slot_hit.astype(jnp.bfloat16)
    send_cells = jnp.sum(jnp.where(slot_hit, station_cell[None, :] + 1, 0), axis=1) - 1
    send_rows = jnp.dot(slot_pick, observations, preferred_element_type=jnp.float32).astype(
        jnp.bfloat16
    )
    got_obs, got_cells = send_out(send_rows, send_cells, lon_count, lat_count, capacity)
    slot_pre = jnp.dot(got_obs, w_station, preferred_element_type=jnp.float32)
    slot_embedded = activate(slot_pre).astype(jnp.bfloat16)
    cell_match = (jnp.arange(tile_cells, dtype=jnp.int32)[:, None] == got_cells[None, :]).astype(
        jnp.bfloat16
    )
    assimilated = jnp.dot(cell_match, slot_embedded, preferred_element_type=jnp.float32)
    state = background.reshape(tile_cells, channels).astype(jnp.float32) + assimilated
    state = state.astype(jnp.bfloat16).reshape(height, breadth, channels)
    state_lat = padded_2(state, (("lat", 0),), 2, False)
    state_rim = padded_2(state_lat, (("lon", 1),), 2, True)
    cotangent_rim = widen(cotangent, 1)
    first_pre = conv_three(state_rim, w_first)
    state_near = state_rim[1:-1, 1:-1].astype(jnp.float32)
    hidden = inside_rows((state_near + activate(first_pre)).astype(jnp.bfloat16))
    encoded = conv_stride(hidden, w_second).astype(jnp.bfloat16)
    hidden_grad = conv_stride_back(cotangent_rim, w_second)
    first_pre_again = lax.optimization_barrier(first_pre)
    first_grad = inside_rows(activate_back(first_pre_again, hidden_grad).astype(jnp.bfloat16))
    state_grad = hidden_grad[1:-1, 1:-1] + conv_three_back(first_grad, w_first)
    state_grad = state_grad.astype(jnp.bfloat16).reshape(tile_cells, channels)
    arrived_grad = lax.dot_general(
        cell_match, state_grad, (((0,), (0,)), ((), ())), preferred_element_type=jnp.float32
    )
    slot_back = activate_back(slot_pre, arrived_grad).astype(jnp.bfloat16)
    slot_grad = lax.dot_general(
        slot_back, w_station, (((1,), (1,)), ((), ())), preferred_element_type=jnp.float32
    ).astype(jnp.bfloat16)
    weight_term = lax.dot_general(
        got_obs, slot_back, (((0,), (0,)), ((), ())), preferred_element_type=jnp.float32
    )
    returned = send_back(slot_grad, lon_count, lat_count, capacity)
    returned, weight_term = lax.optimization_barrier((returned, weight_term))
    station_grad = lax.dot_general(
        slot_pick, returned, (((0,), (0,)), ((), ())), preferred_element_type=jnp.float32
    ).astype(jnp.bfloat16)
    weight_grad = sum_over_devices(weight_term, tile_count)
    weight_grad = weight_grad * (1.0 / math.sqrt(station_count * tile_count))
    return (encoded, station_grad, weight_grad)


def solution(mesh):
    in_specs = (
        P("lat", "lon", None),
        P(("lon", "lat"), None),
        P(),
        P(),
        P(),
        P("lat", "lon", None),
        P(("lon", "lat"), None),
        P(("lon", "lat")),
    )
    out_specs = (P("lat", "lon", None), P(("lon", "lat"), None), P())
    return jax.shard_map(
        on_device, mesh=mesh, in_specs=in_specs, out_specs=out_specs, check_vma=False
    )
```

```python
import math

import jax
import jax.numpy as jnp
from jax import lax
from jax.sharding import PartitionSpec as P

def padded_2(cells, sides, width, closed):
    for axis, dim in sides:
        count = lax.axis_size(axis)
        ends = count if closed else count - 1
        head = lax.slice_in_dim(cells, 0, width, axis=dim)
        tail = lax.slice_in_dim(cells, cells.shape[dim] - width, cells.shape[dim], axis=dim)
        cells = jnp.concatenate(
            [
                lax.ppermute(tail, axis, [(i, (i + 1) % count) for i in range(ends)]),
                cells,
                lax.ppermute(head, axis, [((i + 1) % count, i) for i in range(ends)]),
            ],
            axis=dim,
        )
    return cells


def activate(values):
    return jax.nn.gelu(values, approximate=True)


def activate_back(values, upstream):
    return jax.vjp(activate, values)[1](upstream)[0]


def widen(grid_field, width):
    lon_sides = padded_2(grid_field, (("lon", 1),), width, True)
    return padded_2(lon_sides, (("lat", 0),), width, False)


def inside_rows(field):
    lat_index = lax.axis_index("lat")
    last = lax.axis_size("lat") - 1
    rows = jnp.arange(field.shape[0])[:, None, None]
    outside = ((rows == 0) & (lat_index == 0)) | ((rows == field.shape[0] - 1) & (lat_index == last))
    return jnp.where(outside, jnp.zeros_like(field), field)


def conv_valid(padded, kernel, stride, dilation, spec, rim=0):
    result = lax.conv_general_dilated(
        padded[None],
        kernel,
        (stride, stride),
        ((rim, rim), (rim, rim)),
        lhs_dilation=(dilation, dilation),
        dimension_numbers=("NHWC", spec, "NHWC"),
        preferred_element_type=jnp.float32,
    )
    return result[0]


def conv_three(padded, weight):
    return conv_valid(padded, weight, 1, 1, "HWIO")


def conv_stride(padded, weight):
    return conv_valid(padded, weight, 2, 1, "HWIO")


def conv_three_back(extended, weight):
    return conv_valid(extended, weight[::-1, ::-1], 1, 1, "HWOI")


def conv_stride_back(extended, weight):
    return conv_valid(extended, weight[::-1, ::-1], 1, 2, "HWOI", 1)


def send_out(payload, cell_ids, lon_count, lat_count, capacity):
    feature_width = payload.shape[1]
    got_load, got_cells = (
        lax.all_to_all(
            payload.reshape(lon_count * lat_count, capacity, feature_width),
            ("lon", "lat"),
            split_axis=0,
            concat_axis=0,
            tiled=True,
        ),
        lax.all_to_all(
            cell_ids.reshape(lon_count * lat_count, capacity),
            ("lon", "lat"),
            split_axis=0,
            concat_axis=0,
            tiled=True,
        ),
    )
    return (got_load.reshape(-1, feature_width), got_cells.reshape(-1))


def send_back(reply_rows, lon_count, lat_count, capacity):
    feature_width = reply_rows.shape[1]
    returned = lax.all_to_all(
        reply_rows.reshape(lon_count * lat_count, capacity, feature_width),
        ("lon", "lat"),
        split_axis=0,
        concat_axis=0,
        tiled=True,
    )
    return returned.reshape(-1, feature_width)


def sum_over_devices(term, count):
    rows, width = term.shape
    if rows % count != 0:
        return lax.psum(term, ("lon", "lat"))
    pieces = term.reshape(count, rows // count, width)
    gathered = lax.all_to_all(pieces, ("lon", "lat"), split_axis=0, concat_axis=0, tiled=True)
    own = jnp.sum(gathered, axis=0, keepdims=True)
    spread = jnp.broadcast_to(own, (count, rows // count, width))
    whole = lax.all_to_all(spread, ("lon", "lat"), split_axis=0, concat_axis=0, tiled=True)
    return whole.reshape(rows, width)


def on_device(
    background, observations, w_station, w_first, w_second, cotangent, station_tile, station_cell
):
    lon_count = lax.axis_size("lon")
    lat_count = lax.axis_size("lat")
    tile_count = lon_count * lat_count
    height, breadth, channels = background.shape
    tile_cells = height * breadth
    station_count = observations.shape[0]
    capacity = 2 * station_count // tile_count
    slot_total = tile_count * capacity
    target_tile = station_tile[:, 0]
    matches = (target_tile[:, None] == jnp.arange(tile_count, dtype=jnp.int32)[None, :]).astype(
        jnp.bfloat16
    )
    order = jnp.arange(station_count, dtype=jnp.int32)
    before = (order[:, None] > order[None, :]).astype(jnp.bfloat16)
    earlier = jnp.dot(before, matches, preferred_element_type=jnp.float32)
    rank = jnp.sum(earlier * matches.astype(jnp.float32), axis=1).astype(jnp.int32)
    flat_slot = target_tile * capacity + rank
    slot_hit = jnp.arange(slot_total, dtype=jnp.int32)[:, None] == flat_slot[None, :]
    slot_pick = slot_hit.astype(jnp.bfloat16)
    send_cells = jnp.sum(jnp.where(slot_hit, station_cell[None, :] + 1, 0), axis=1) - 1
    send_rows = jnp.dot(slot_pick, observations, preferred_element_type=jnp.float32).astype(
        jnp.bfloat16
    )
    got_obs, got_cells = send_out(send_rows, send_cells, lon_count, lat_count, capacity)
    slot_pre = jnp.dot(got_obs, w_station, preferred_element_type=jnp.float32)
    slot_embedded = activate(slot_pre).astype(jnp.bfloat16)
    cell_match = (jnp.arange(tile_cells, dtype=jnp.int32)[:, None] == got_cells[None, :]).astype(
        jnp.bfloat16
    )
    assimilated = jnp.dot(cell_match, slot_embedded, preferred_element_type=jnp.float32)
    state = background.reshape(tile_cells, channels).astype(jnp.float32) + assimilated
    state = state.astype(jnp.bfloat16).reshape(height, breadth, channels)
    state_lat = padded_2(state, (("lat", 0),), 2, False)
    state_rim = padded_2(state_lat, (("lon", 1),), 2, True)
    cotangent_lat = padded_2(cotangent, (("lat", 0),), 1, False)
    cotangent_rim = padded_2(cotangent_lat, (("lon", 1),), 1, True)
    first_pre = conv_three(state_rim, w_first)
    state_near = state_rim[1:-1, 1:-1].astype(jnp.float32)
    hidden = inside_rows((state_near + activate(first_pre)).astype(jnp.bfloat16))
    encoded = conv_stride(hidden, w_second).astype(jnp.bfloat16)
    hidden_grad = conv_stride_back(cotangent_rim, w_second)
    first_pre_again = lax.optimization_barrier(first_pre)
    first_grad = inside_rows(activate_back(first_pre_again, hidden_grad).astype(jnp.bfloat16))
    state_grad = hidden_grad[1:-1, 1:-1] + conv_three_back(first_grad, w_first)
    state_grad = state_grad.astype(jnp.bfloat16).reshape(tile_cells, channels)
    arrived_grad = lax.dot_general(
        cell_match, state_grad, (((0,), (0,)), ((), ())), preferred_element_type=jnp.float32
    )
    slot_back = activate_back(slot_pre, arrived_grad).astype(jnp.bfloat16)
    slot_grad = lax.dot_general(
        slot_back, w_station, (((1,), (1,)), ((), ())), preferred_element_type=jnp.float32
    ).astype(jnp.bfloat16)
    weight_term = lax.dot_general(
        got_obs, slot_back, (((0,), (0,)), ((), ())), preferred_element_type=jnp.float32
    )
    returned = send_back(slot_grad, lon_count, lat_count, capacity)
    returned, weight_term = lax.optimization_barrier((returned, weight_term))
    station_grad = lax.dot_general(
        slot_pick, returned, (((0,), (0,)), ((), ())), preferred_element_type=jnp.float32
    ).astype(jnp.bfloat16)
    weight_grad = sum_over_devices(weight_term, tile_count)
    weight_grad = weight_grad * (1.0 / math.sqrt(station_count * tile_count))
    return (encoded, station_grad, weight_grad)


def solution(mesh):
    in_specs = (
        P("lat", "lon", None),
        P(("lon", "lat"), None),
        P(),
        P(),
        P(),
        P("lat", "lon", None),
        P(("lon", "lat"), None),
        P(("lon", "lat")),
    )
    out_specs = (P("lat", "lon", None), P(("lon", "lat"), None), P())
    return jax.shard_map(
        on_device, mesh=mesh, in_specs=in_specs, out_specs=out_specs, check_vma=False
    )
```

```python
import math

import jax
import jax.numpy as jnp
from jax import lax
from jax.sharding import PartitionSpec as P

def padded_2(cells, sides, width, closed):
    for axis, dim in sides:
        count = lax.axis_size(axis)
        ends = count if closed else count - 1
        head = lax.slice_in_dim(cells, 0, width, axis=dim)
        tail = lax.slice_in_dim(cells, cells.shape[dim] - width, cells.shape[dim], axis=dim)
        cells = jnp.concatenate(
            [
                lax.ppermute(tail, axis, [(i, (i + 1) % count) for i in range(ends)]),
                cells,
                lax.ppermute(head, axis, [((i + 1) % count, i) for i in range(ends)]),
            ],
            axis=dim,
        )
    return cells


def activate(values):
    return jax.nn.gelu(values, approximate=True)


def activate_back(values, upstream):
    return jax.vjp(activate, values)[1](upstream)[0]


def widen(grid_field, width):
    lon_sides = padded_2(grid_field, (("lon", 1),), width, True)
    return padded_2(lon_sides, (("lat", 0),), width, False)


def inside_rows(field):
    lat_index = lax.axis_index("lat")
    last = lax.axis_size("lat") - 1
    rows = jnp.arange(field.shape[0])[:, None, None]
    outside = ((rows == 0) & (lat_index == 0)) | ((rows == field.shape[0] - 1) & (lat_index == last))
    return jnp.where(outside, jnp.zeros_like(field), field)


def conv_valid(padded, kernel, stride, dilation, spec, rim=0):
    result = lax.conv_general_dilated(
        padded[None],
        kernel,
        (stride, stride),
        ((rim, rim), (rim, rim)),
        lhs_dilation=(dilation, dilation),
        dimension_numbers=("NHWC", spec, "NHWC"),
        preferred_element_type=jnp.float32,
    )
    return result[0]


def conv_three(padded, weight):
    return conv_valid(padded, weight, 1, 1, "HWIO")


def conv_stride(padded, weight):
    return conv_valid(padded, weight, 2, 1, "HWIO")


def conv_three_back(extended, weight):
    return conv_valid(extended, weight[::-1, ::-1], 1, 1, "HWOI")


def conv_stride_back(extended, weight):
    return conv_valid(extended, weight[::-1, ::-1], 1, 2, "HWOI", 1)


def send_out(payload, cell_ids, lon_count, lat_count, capacity):
    feature_width = payload.shape[1]
    got_load, got_cells = (
        lax.all_to_all(
            payload.reshape(lon_count * lat_count, capacity, feature_width),
            ("lon", "lat"),
            split_axis=0,
            concat_axis=0,
            tiled=True,
        ),
        lax.all_to_all(
            cell_ids.reshape(lon_count * lat_count, capacity),
            ("lon", "lat"),
            split_axis=0,
            concat_axis=0,
            tiled=True,
        ),
    )
    return (got_load.reshape(-1, feature_width), got_cells.reshape(-1))


def send_back(reply_rows, lon_count, lat_count, capacity):
    feature_width = reply_rows.shape[1]
    returned = lax.all_to_all(
        reply_rows.reshape(lon_count * lat_count, capacity, feature_width),
        ("lon", "lat"),
        split_axis=0,
        concat_axis=0,
        tiled=True,
    )
    return returned.reshape(-1, feature_width)


def sum_over_devices(term, count, scale):
    rows, width = term.shape
    if rows % count != 0:
        return lax.psum(term, ("lon", "lat")) * scale
    pieces = term.reshape(count, rows // count, width)
    gathered = lax.all_to_all(pieces, ("lon", "lat"), split_axis=0, concat_axis=0, tiled=True)
    own = jnp.sum(gathered, axis=0, keepdims=True) * scale
    spread = jnp.broadcast_to(own, (count, rows // count, width))
    whole = lax.all_to_all(spread, ("lon", "lat"), split_axis=0, concat_axis=0, tiled=True)
    return whole.reshape(rows, width)


def on_device(
    background, observations, w_station, w_first, w_second, cotangent, station_tile, station_cell
):
    lon_count = lax.axis_size("lon")
    lat_count = lax.axis_size("lat")
    tile_count = lon_count * lat_count
    height, breadth, channels = background.shape
    tile_cells = height * breadth
    station_count = observations.shape[0]
    capacity = 2 * station_count // tile_count
    slot_total = tile_count * capacity
    target_tile = station_tile[:, 0]
    matches = (target_tile[:, None] == jnp.arange(tile_count, dtype=jnp.int32)[None, :]).astype(
        jnp.bfloat16
    )
    order = jnp.arange(station_count, dtype=jnp.int32)
    before = (order[:, None] > order[None, :]).astype(jnp.bfloat16)
    earlier = jnp.dot(before, matches, preferred_element_type=jnp.float32)
    rank = jnp.sum(earlier * matches.astype(jnp.float32), axis=1).astype(jnp.int32)
    flat_slot = target_tile * capacity + rank
    slot_hit = jnp.arange(slot_total, dtype=jnp.int32)[:, None] == flat_slot[None, :]
    slot_pick = slot_hit.astype(jnp.bfloat16)
    send_cells = jnp.sum(jnp.where(slot_hit, station_cell[None, :] + 1, 0), axis=1) - 1
    send_rows = jnp.dot(slot_pick, observations, preferred_element_type=jnp.float32).astype(
        jnp.bfloat16
    )
    got_obs, got_cells = send_out(send_rows, send_cells, lon_count, lat_count, capacity)
    slot_pre = jnp.dot(got_obs, w_station, preferred_element_type=jnp.float32)
    slot_embedded = activate(slot_pre).astype(jnp.bfloat16)
    cell_match = (jnp.arange(tile_cells, dtype=jnp.int32)[:, None] == got_cells[None, :]).astype(
        jnp.bfloat16
    )
    assimilated = jnp.dot(cell_match, slot_embedded, preferred_element_type=jnp.float32)
    state = background.reshape(tile_cells, channels).astype(jnp.float32) + assimilated
    state = state.astype(jnp.bfloat16).reshape(height, breadth, channels)
    state_lat = padded_2(state, (("lat", 0),), 2, False)
    state_rim = padded_2(state_lat, (("lon", 1),), 2, True)
    cotangent_rim = widen(cotangent, 1)
    first_pre = conv_three(state_rim, w_first)
    state_near = state_rim[1:-1, 1:-1].astype(jnp.float32)
    hidden = inside_rows((state_near + activate(first_pre)).astype(jnp.bfloat16))
    encoded = conv_stride(hidden, w_second).astype(jnp.bfloat16)
    hidden_grad = conv_stride_back(cotangent_rim, w_second)
    first_pre_again = lax.optimization_barrier(first_pre)
    first_grad = inside_rows(activate_back(first_pre_again, hidden_grad).astype(jnp.bfloat16))
    state_grad = hidden_grad[1:-1, 1:-1] + conv_three_back(first_grad, w_first)
    state_grad = state_grad.astype(jnp.bfloat16).reshape(tile_cells, channels)
    arrived_grad = lax.dot_general(
        cell_match, state_grad, (((0,), (0,)), ((), ())), preferred_element_type=jnp.float32
    )
    slot_back = activate_back(slot_pre, arrived_grad).astype(jnp.bfloat16)
    slot_grad = lax.dot_general(
        slot_back, w_station, (((1,), (1,)), ((), ())), preferred_element_type=jnp.float32
    ).astype(jnp.bfloat16)
    weight_term = lax.dot_general(
        got_obs, slot_back, (((0,), (0,)), ((), ())), preferred_element_type=jnp.float32
    )
    returned = send_back(slot_grad, lon_count, lat_count, capacity)
    returned, weight_term = lax.optimization_barrier((returned, weight_term))
    station_grad = lax.dot_general(
        slot_pick, returned, (((0,), (0,)), ((), ())), preferred_element_type=jnp.float32
    ).astype(jnp.bfloat16)
    weight_grad = sum_over_devices(
        weight_term, tile_count, 1.0 / math.sqrt(station_count * tile_count)
    )
    return (encoded, station_grad, weight_grad)


def solution(mesh):
    in_specs = (
        P("lat", "lon", None),
        P(("lon", "lat"), None),
        P(),
        P(),
        P(),
        P("lat", "lon", None),
        P(("lon", "lat"), None),
        P(("lon", "lat")),
    )
    out_specs = (P("lat", "lon", None), P(("lon", "lat"), None), P())
    return jax.shard_map(
        on_device, mesh=mesh, in_specs=in_specs, out_specs=out_specs, check_vma=False
    )
```

```python
import math

import jax
import jax.numpy as jnp
from jax import lax
from jax.sharding import PartitionSpec as P

def padded_2(cells, sides, width, closed):
    for axis, dim in sides:
        count = lax.axis_size(axis)
        ends = count if closed else count - 1
        head = lax.slice_in_dim(cells, 0, width, axis=dim)
        tail = lax.slice_in_dim(cells, cells.shape[dim] - width, cells.shape[dim], axis=dim)
        cells = jnp.concatenate(
            [
                lax.ppermute(tail, axis, [(i, (i + 1) % count) for i in range(ends)]),
                cells,
                lax.ppermute(head, axis, [((i + 1) % count, i) for i in range(ends)]),
            ],
            axis=dim,
        )
    return cells


def activate(values):
    return jax.nn.gelu(values, approximate=True)


def activate_back(values, upstream):
    return jax.vjp(activate, values)[1](upstream)[0]


def widen(grid_field, width):
    lon_sides = padded_2(grid_field, (("lon", 1),), width, True)
    return padded_2(lon_sides, (("lat", 0),), width, False)


def inside_rows(field):
    lat_index = lax.axis_index("lat")
    last = lax.axis_size("lat") - 1
    rows = jnp.arange(field.shape[0])[:, None, None]
    outside = ((rows == 0) & (lat_index == 0)) | ((rows == field.shape[0] - 1) & (lat_index == last))
    return jnp.where(outside, jnp.zeros_like(field), field)


def conv_valid(padded, kernel, stride, dilation, spec, rim=0):
    result = lax.conv_general_dilated(
        padded[None],
        kernel,
        (stride, stride),
        ((rim, rim), (rim, rim)),
        lhs_dilation=(dilation, dilation),
        dimension_numbers=("NHWC", spec, "NHWC"),
        preferred_element_type=jnp.float32,
    )
    return result[0]


def conv_three(padded, weight):
    return conv_valid(padded, weight, 1, 1, "HWIO")


def conv_stride(padded, weight):
    return conv_valid(padded, weight, 2, 1, "HWIO")


def conv_three_back(extended, weight):
    return conv_valid(extended, weight[::-1, ::-1], 1, 1, "HWOI")


def conv_stride_back(extended, weight):
    return conv_valid(extended, weight[::-1, ::-1], 1, 2, "HWOI", 1)


def send_out(payload, cell_ids, lon_count, lat_count, capacity):
    feature_width = payload.shape[1]
    got_load, got_cells = (
        lax.all_to_all(
            payload.reshape(lon_count * lat_count, capacity, feature_width),
            ("lon", "lat"),
            split_axis=0,
            concat_axis=0,
            tiled=True,
        ),
        lax.all_to_all(
            cell_ids.reshape(lon_count * lat_count, capacity),
            ("lon", "lat"),
            split_axis=0,
            concat_axis=0,
            tiled=True,
        ),
    )
    return (got_load.reshape(-1, feature_width), got_cells.reshape(-1))


def send_back(reply_rows, lon_count, lat_count, capacity):
    feature_width = reply_rows.shape[1]
    returned = lax.all_to_all(
        reply_rows.reshape(lon_count * lat_count, capacity, feature_width),
        ("lon", "lat"),
        split_axis=0,
        concat_axis=0,
        tiled=True,
    )
    return returned.reshape(-1, feature_width)


def split_rows(term, count):
    rows, width = term.shape
    if rows % count != 0:
        return term
    return term.reshape(count, rows // count, width)


def sum_over_devices(pieces, count):
    if pieces.ndim == 2:
        return lax.psum(pieces, ("lon", "lat"))
    rows, width = pieces.shape[0] * pieces.shape[1], pieces.shape[2]
    gathered = lax.all_to_all(pieces, ("lon", "lat"), split_axis=0, concat_axis=0, tiled=True)
    own = jnp.sum(gathered, axis=0, keepdims=True)
    spread = jnp.broadcast_to(own, (count, rows // count, width))
    whole = lax.all_to_all(spread, ("lon", "lat"), split_axis=0, concat_axis=0, tiled=True)
    return whole.reshape(rows, width)


def on_device(
    background, observations, w_station, w_first, w_second, cotangent, station_tile, station_cell
):
    lon_count = lax.axis_size("lon")
    lat_count = lax.axis_size("lat")
    tile_count = lon_count * lat_count
    height, breadth, channels = background.shape
    tile_cells = height * breadth
    station_count = observations.shape[0]
    capacity = 2 * station_count // tile_count
    slot_total = tile_count * capacity
    target_tile = station_tile[:, 0]
    matches = (target_tile[:, None] == jnp.arange(tile_count, dtype=jnp.int32)[None, :]).astype(
        jnp.bfloat16
    )
    order = jnp.arange(station_count, dtype=jnp.int32)
    before = (order[:, None] > order[None, :]).astype(jnp.bfloat16)
    earlier = jnp.dot(before, matches, preferred_element_type=jnp.float32)
    rank = jnp.sum(earlier * matches.astype(jnp.float32), axis=1).astype(jnp.int32)
    flat_slot = target_tile * capacity + rank
    slot_hit = jnp.arange(slot_total, dtype=jnp.int32)[:, None] == flat_slot[None, :]
    slot_pick = slot_hit.astype(jnp.bfloat16)
    send_cells = jnp.sum(jnp.where(slot_hit, station_cell[None, :] + 1, 0), axis=1) - 1
    send_rows = jnp.dot(slot_pick, observations, preferred_element_type=jnp.float32).astype(
        jnp.bfloat16
    )
    got_obs, got_cells = send_out(send_rows, send_cells, lon_count, lat_count, capacity)
    slot_pre = jnp.dot(got_obs, w_station, preferred_element_type=jnp.float32)
    slot_embedded = activate(slot_pre).astype(jnp.bfloat16)
    cell_match = (jnp.arange(tile_cells, dtype=jnp.int32)[:, None] == got_cells[None, :]).astype(
        jnp.bfloat16
    )
    assimilated = jnp.dot(cell_match, slot_embedded, preferred_element_type=jnp.float32)
    state = background.reshape(tile_cells, channels).astype(jnp.float32) + assimilated
    state = state.astype(jnp.bfloat16).reshape(height, breadth, channels)
    state_lat = padded_2(state, (("lat", 0),), 2, False)
    state_rim = padded_2(state_lat, (("lon", 1),), 2, True)
    cotangent_rim = widen(cotangent, 1)
    first_pre = conv_three(state_rim, w_first)
    state_near = state_rim[1:-1, 1:-1].astype(jnp.float32)
    hidden = inside_rows((state_near + activate(first_pre)).astype(jnp.bfloat16))
    encoded = conv_stride(hidden, w_second).astype(jnp.bfloat16)
    hidden_grad = conv_stride_back(cotangent_rim, w_second)
    first_pre_again = lax.optimization_barrier(first_pre)
    first_grad = inside_rows(activate_back(first_pre_again, hidden_grad).astype(jnp.bfloat16))
    state_grad = hidden_grad[1:-1, 1:-1] + conv_three_back(first_grad, w_first)
    state_grad = state_grad.astype(jnp.bfloat16).reshape(tile_cells, channels)
    arrived_grad = lax.dot_general(
        cell_match, state_grad, (((0,), (0,)), ((), ())), preferred_element_type=jnp.float32
    )
    slot_back = activate_back(slot_pre, arrived_grad).astype(jnp.bfloat16)
    slot_grad = lax.dot_general(
        slot_back, w_station, (((1,), (1,)), ((), ())), preferred_element_type=jnp.float32
    ).astype(jnp.bfloat16)
    weight_term = lax.dot_general(
        got_obs, slot_back, (((0,), (0,)), ((), ())), preferred_element_type=jnp.float32
    )
    returned = send_back(slot_grad, lon_count, lat_count, capacity)
    weight_term = split_rows(weight_term, tile_count)
    returned, weight_term = lax.optimization_barrier((returned, weight_term))
    station_grad = lax.dot_general(
        slot_pick, returned, (((0,), (0,)), ((), ())), preferred_element_type=jnp.float32
    ).astype(jnp.bfloat16)
    weight_grad = sum_over_devices(weight_term, tile_count)
    weight_grad = weight_grad * (1.0 / math.sqrt(station_count * tile_count))
    return (encoded, station_grad, weight_grad)


def solution(mesh):
    in_specs = (
        P("lat", "lon", None),
        P(("lon", "lat"), None),
        P(),
        P(),
        P(),
        P("lat", "lon", None),
        P(("lon", "lat"), None),
        P(("lon", "lat")),
    )
    out_specs = (P("lat", "lon", None), P(("lon", "lat"), None), P())
    return jax.shard_map(
        on_device, mesh=mesh, in_specs=in_specs, out_specs=out_specs, check_vma=False
    )
```
